256 devices in a mesh: shot: 16 (over y, x_lo, core), space: 16 (over z, x_hi).
Axes of the slice: x: 4 (x_hi: 2, x_lo: 2; x = x_hi * 2 + x_lo), y: 4, z: 8, core: 2. Of those that a mesh axis runs over, the one named last changes fastest.
Arguments:
- courant: float32 [128, 128, 128], P('space'), may hold values from 0.03 to 0.18
- checkpoint: float32 [16, 2, 2048, 8, 128], P('shot', None, 'space'), may hold values from -6 to 6
- block_target: int32 [16, 2048], P('shot'), may hold values from 0 to 2047, as said below
- adjoint_state: float32 [16, 2, 128, 128, 128], P('shot', None, 'space'), may hold values from -6 to 6
- wavelet: float32 [16, 4], P('shot'), may hold values from -8 to 8
- source_cell: int32 [16], P('shot'), may hold values from 0 to 2097151
- receiver_cell: int32 [16, 512], P('shot'), may hold values from 0 to 2097151
- residual: float32 [16, 4, 512], P('shot'), may hold values from -6 to 6
- check_rows: int32 [16, 128, 16], P('space'), may hold values from 0 to 1023
Outputs:
- gradient: float32 [128, 128, 128], P('space', 'shot')
- adjoint_carry: float32 [16, 2, 128, 128, 128], P('shot', None, 'space')
- checksums: float32 [16, 128, 128], P('space', 'shot')
The draws below stay inside these ranges and needn't reach their ends.
Inputs may be any that keep to these rules, and one draw needn't show every extreme that they name: `block_target`: each shot's row is a permutation of the block positions. The stored blocks of one device (aligned blocks of 128 entries) name at most 32 positions of any one slab (128 consecutive positions); each device names exactly 32 of one slab, and each slab is named exactly 32 times by one device.
All inputs are finite; a program needn't handle non-finite values.
Results may differ from the reference program's by a relative error of at most 0.0003.
Values sent between devices are 32-bit elements; how exact they have to be, the bound alone decides.
No kernel may reach another device: no remote copies, remote signals or barrier semaphores. Data moves between devices by JAX's collectives and lax.ppermute only.
A program may use at most 128 MiB of HBM per device.

```python
import math
import jax
import jax.numpy as jnp
from jax import lax

CX = 8
NY = 128
NZ = 128
NREC = 512
BY = 8
NT = 4
KSEL = 16
NX = 128
SHOTS = 16
BLK_DEV = 128
NBLK = 2048
CAP = 32
CHK_SLAB = 128
N_SPACE = 16


def one_target(subkey):
    readers = NBLK // BLK_DEV
    key_shift, key_read, key_send = jax.random.split(subkey, 3)
    shifts = jax.random.permutation(key_shift, readers)
    remainder = BLK_DEV - CAP
    ranking = jnp.arange(readers, dtype=jnp.int32)
    weights = jnp.where(ranking == 0, CAP, remainder // (readers - 1) + (ranking - 1 < remainder % (readers - 1)).astype(jnp.int32)).astype(jnp.int32)
    by_shift = jnp.zeros((readers,), jnp.int32).at[shifts].set(weights)
    senders = jnp.arange(readers, dtype=jnp.int32)
    counts = by_shift[(senders[None, :] - senders[:, None]) % readers]
    send_end = jnp.cumsum(counts, axis=1)
    send_start = send_end - counts
    take_end = jnp.cumsum(counts, axis=0)
    take_start = take_end - counts
    slot_ids = jnp.arange(BLK_DEV, dtype=jnp.int32)
    peer_of = jnp.sum((send_end[:, None, :] <= slot_ids[None, :, None]).astype(jnp.int32), axis=2)
    within = slot_ids[None, :] - jnp.take_along_axis(send_start, peer_of, axis=1)
    arrival = jnp.take_along_axis(take_start, peer_of, axis=1) + within
    read_perm = jax.vmap(lambda subject: jax.random.permutation(subject, BLK_DEV))(jax.random.split(key_read, readers))
    send_perm = jax.vmap(lambda subject: jax.random.permutation(subject, BLK_DEV))(jax.random.split(key_send, readers))
    local_block = read_perm[peer_of, arrival]
    global_block = peer_of * BLK_DEV + local_block
    placed = jnp.zeros((readers, BLK_DEV), jnp.int32).at[senders[:, None], send_perm].set(global_block.astype(jnp.int32))
    return placed.reshape(-1)


def draw_block_target(key, part):
    return jax.vmap(one_target)(jax.random.split(key, SHOTS))


def plant(values, own_key, low, top_value):
    dims = values.shape
    place = [jax.random.randint(jax.random.fold_in(own_key, axis), (), 0, dims[axis]) for axis in range(len(dims))]
    values = values.at[tuple(place)].set(low)
    longest = dims.index(max(dims))
    place[longest] = (place[longest] + 1) % dims[longest]
    return values.at[tuple(place)].set(top_value)


def shard_levels(own_key, shape, cuts, least, top_value):
    def one(axis_at, parts):
        heights = jax.random.uniform(jax.random.fold_in(jax.random.fold_in(own_key, 6), axis_at), (parts,), jnp.float32, least / len(cuts), top_value / len(cuts))
        return jnp.repeat(jnp.exp(heights), shape[axis_at] // parts).reshape((-1,) + (1,) * (len(shape) - axis_at - 1))

    factor_of = one(*cuts[0])
    for cut in cuts[1:]:
        factor_of = factor_of * one(*cut)
    return factor_of


def noise(own_key, extent, width, limit, shards=(), kind=jnp.bfloat16):
    loudness = shard_levels(own_key, extent, shards, -0.22, 0.18) if shards else 1.0
    values = jax.random.normal(own_key, extent, jnp.float32) * width * loudness
    return jnp.minimum(jnp.maximum(values, -limit), limit).astype(kind)


def setup_inputs(seed: int = 0) -> dict:
    streams_of = jax.random.split(jax.random.key(seed), 10)
    return {
        "courant": jnp.clip(jnp.exp(math.log(0.18) - 1.7917595 * jax.random.uniform(streams_of[0], (NX, NY, NZ), jnp.float32) ** shard_levels(streams_of[0], (NX, NY, NZ), ((0, 16),), -0.2, 0.2)), 0.03, 0.18),
        "checkpoint": noise(streams_of[1], (SHOTS, 2, NBLK, BY, NZ), 1.0, 6.0, ((0, 16), (2, 16)), jnp.float32),
        "block_target": draw_block_target(jax.random.fold_in(streams_of[9], 71), 0),
        "adjoint_state": noise(streams_of[3], (SHOTS, 2, NX, NY, NZ), 1.0, 6.0, ((0, 16), (2, 16)), jnp.float32),
        "wavelet": noise(streams_of[4], (SHOTS, NT), 2.0, 8.0, ((0, 16),), jnp.float32),
        "source_cell": plant(jax.random.randint(streams_of[5], (SHOTS,), 0, NX * NY * NZ), jax.random.fold_in(streams_of[5], 1), 0, (NX * NY * NZ) - 1).astype(jnp.int32),
        "receiver_cell": plant(jax.random.randint(streams_of[6], (SHOTS, NREC), 0, NX * NY * NZ), jax.random.fold_in(streams_of[6], 1), 0, (NX * NY * NZ) - 1).astype(jnp.int32),
        "residual": noise(streams_of[7], (SHOTS, NT, NREC), 1.0, 6.0, ((0, 16),), jnp.float32),
        "check_rows": plant(jax.random.randint(streams_of[8], (N_SPACE, CHK_SLAB, KSEL), 0, CX * NY), jax.random.fold_in(streams_of[8], 1), 0, (CX * NY) - 1).astype(jnp.int32),
    }


STENCIL = (-205.0 / 72.0, 8.0 / 5.0, -1.0 / 5.0, 8.0 / 315.0, -1.0 / 560.0)


def laplace(field):
    length = field.shape[0] - 8
    height = field.shape[1]
    breadth = field.shape[2]
    padded = jnp.pad(field, ((0, 0), (4, 4), (4, 4)))
    summed = (3.0 * STENCIL[0]) * padded[4:4 + length, 4:4 + height, 4:4 + breadth]
    for offset in range(1, 5):
        summed = summed + STENCIL[offset] * (padded[4 + offset:4 + offset + length, 4:4 + height, 4:4 + breadth] + padded[4 - offset:4 - offset + length, 4:4 + height, 4:4 + breadth])
    for offset in range(1, 5):
        summed = summed + STENCIL[offset] * (padded[4:4 + length, 4 + offset:4 + offset + height, 4:4 + breadth] + padded[4:4 + length, 4 - offset:4 - offset + height, 4:4 + breadth])
    for offset in range(1, 5):
        summed = summed + STENCIL[offset] * (padded[4:4 + length, 4:4 + height, 4 + offset:4 + offset + breadth] + padded[4:4 + length, 4:4 + height, 4 - offset:4 - offset + breadth])
    return summed


def inject(field, cell_index, values, first_row):
    plane_cells = field.shape[1] * field.shape[2]
    local_cell = cell_index - first_row * plane_cells
    inside = (local_cell >= 0) & (local_cell < field.shape[0] * plane_cells)
    target = jnp.where(inside, local_cell, field.shape[0] * plane_cells)
    flattened = field.reshape(-1).at[target].add(values, mode="drop")
    return flattened.reshape(field.shape)


def advance(before, current_ext, courant, wave_value, source, first_row):
    following = 2.0 * current_ext[4:-4] - before + courant * laplace(current_ext)
    return inject(following, source, wave_value, first_row)


def retreat(following, current, weighted_ext, values, cell_index, first_row):
    earlier = 2.0 * current - following + laplace(weighted_ext)
    return inject(earlier, cell_index, values, first_row)


def pad_planes(field):
    return jnp.pad(field, ((4, 4), (0, 0), (0, 0)))


def pick_sum(slab_rows, chosen):
    return jnp.sum(slab_rows[chosen], axis=1)


def reference(courant, checkpoint, block_target, adjoint_state, wavelet, source_cell, receiver_cell, residual, check_rows):
    def one_shot(running, inputs):
        blocks, target, carried, wavelet_row, source, receivers, traces = inputs
        placed = jnp.zeros_like(blocks).at[:, target].set(blocks)
        levels = placed.reshape(2, NX, NY, NZ)
        fields = [levels[0], levels[1]]
        for moment in range(1, NT + 1):
            fields.append(advance(fields[-2], pad_planes(fields[-1]), courant, wavelet_row[moment - 1:moment], source.reshape(1), 0))
        adjoints = [None] * (NT + 2)
        adjoints[NT + 1] = carried[0]
        adjoints[NT] = carried[1]
        for moment in range(NT, 0, -1):
            weighted = pad_planes(courant * adjoints[moment])
            adjoints[moment - 1] = retreat(adjoints[moment + 1], adjoints[moment], weighted, traces[moment - 1], receivers, 0)
        partial_value = jnp.zeros((NX, NY, NZ), jnp.float32)
        for moment in range(1, NT + 1):
            partial_value = partial_value + adjoints[moment] * ((fields[moment + 1] - 2.0 * fields[moment]) + fields[moment - 1])
        return running + partial_value, jnp.stack([adjoints[1], adjoints[0]])

    gradient, adjoint_carry = lax.scan(one_shot, jnp.zeros((NX, NY, NZ), jnp.float32), (checkpoint, block_target, adjoint_state, wavelet, source_cell, receiver_cell, residual))
    slab_view = gradient.reshape(N_SPACE, CX * NY, NZ)
    checksums = jax.vmap(pick_sum)(slab_view, check_rows)
    return gradient, adjoint_carry, checksums
```

```python
import jax
import jax.numpy as jnp
from jax import lax
from jax.sharding import PartitionSpec as P

STENCIL = (-205.0 / 72.0, 8.0 / 5.0, -1.0 / 5.0, 8.0 / 315.0, -1.0 / 560.0)


def padded_2(array, sides, width):
    for axis, dim in sides:
        devices, length = (lax.axis_size(axis), array.shape[dim])
        up = [(i, (i + 1) % devices) for i in range(devices - 1)]
        down = [(j, i) for i, j in up]
        last = lax.slice_in_dim(array, length - width, length, axis=dim)
        initial = lax.slice_in_dim(array, 0, width, axis=dim)
        before = lax.ppermute(last, axis, up)
        after = lax.ppermute(initial, axis, down)
        array = jnp.concatenate([before, array, after], axis=dim)
    return array


def laplace(field):
    length = field.shape[0] - 8
    height = field.shape[1]
    breadth = field.shape[2]
    padded = jnp.pad(field, ((0, 0), (4, 4), (4, 4)))
    summed = 3.0 * STENCIL[0] * padded[4 : 4 + length, 4 : 4 + height, 4 : 4 + breadth]
    for offset in range(1, 5):
        summed = summed + STENCIL[offset] * (
            padded[4 + offset : 4 + offset + length, 4 : 4 + height, 4 : 4 + breadth]
            + padded[4 - offset : 4 - offset + length, 4 : 4 + height, 4 : 4 + breadth]
        )
    for offset in range(1, 5):
        summed = summed + STENCIL[offset] * (
            padded[4 : 4 + length, 4 + offset : 4 + offset + height, 4 : 4 + breadth]
            + padded[4 : 4 + length, 4 - offset : 4 - offset + height, 4 : 4 + breadth]
        )
    for offset in range(1, 5):
        summed = summed + STENCIL[offset] * (
            padded[4 : 4 + length, 4 : 4 + height, 4 + offset : 4 + offset + breadth]
            + padded[4 : 4 + length, 4 : 4 + height, 4 - offset : 4 - offset + breadth]
        )
    return summed


def inject(field, cell_index, values, first_row):
    plane_cells = field.shape[1] * field.shape[2]
    local_cell = cell_index - first_row * plane_cells
    inside = (local_cell >= 0) & (local_cell < field.shape[0] * plane_cells)
    target = jnp.where(inside, local_cell, field.shape[0] * plane_cells)
    flattened = field.reshape(-1).at[target].add(values, mode="drop")
    return flattened.reshape(field.shape)


def inject_dense(field, cell_index, values, first_row):
    plane_cells = field.shape[1] * field.shape[2]
    local_cell = cell_index[0] - first_row * plane_cells
    cells = (
        lax.broadcasted_iota(jnp.int32, field.shape, 0) * plane_cells
        + lax.broadcasted_iota(jnp.int32, field.shape, 1) * field.shape[2]
        + lax.broadcasted_iota(jnp.int32, field.shape, 2)
    )
    return field + jnp.where(cells == local_cell, values[0], 0.0)


def advance(before, current_ext, courant, wave_value, source, first_row):
    following = 2.0 * current_ext[4:-4] - before + courant * laplace(current_ext)
    return inject_dense(following, source, wave_value, first_row)


def retreat(following, current, weighted_ext, values, cell_index, first_row):
    earlier = 2.0 * current - following + laplace(weighted_ext)
    return inject(earlier, cell_index, values, first_row)


def extend(field):
    return padded_2(field, (("space", 0),), 4)


def body(
    courant,
    checkpoint,
    block_target,
    adjoint_state,
    wavelet,
    source_cell,
    receiver_cell,
    residual,
    check_rows,
):
    devices = lax.axis_size("space")
    position = lax.axis_index("space")
    length, height, breadth = courant.shape
    first_row = position * length
    per_device = checkpoint.shape[2]
    block_rows = checkpoint.shape[3]
    capacity = per_device // 4
    targets = block_target[0]
    payload = checkpoint[0]
    peers = targets // per_device
    matches = (peers[:, None] == jnp.arange(devices, dtype=jnp.int32)[None, :]).astype(jnp.int32)
    grouped = matches.reshape(devices, per_device, devices)
    ranking = jnp.sum((jnp.cumsum(grouped, axis=1) - grouped) * grouped, axis=2)
    peer_grid = peers.reshape(devices, per_device)
    own_peers = lax.dynamic_index_in_dim(peer_grid, position, 0, keepdims=False)
    own_ranks = lax.dynamic_index_in_dim(ranking, position, 0, keepdims=False)
    slot_of = own_peers * capacity + own_ranks
    outgoing = (
        jnp.zeros((2, devices * capacity, block_rows, breadth), jnp.float32)
        .at[:, slot_of]
        .set(payload)
    )
    outgoing = outgoing.reshape(2, devices, capacity, block_rows, breadth)
    incoming = lax.all_to_all(outgoing, "space", split_axis=1, concat_axis=1, tiled=True)
    incoming = incoming.reshape(2, devices * capacity, block_rows, breadth)
    sender_grid = jnp.arange(devices, dtype=jnp.int32)[:, None] * capacity + ranking
    owned = peer_grid == position
    local_block = (targets % per_device).reshape(devices, per_device)
    where_from = (
        jnp.zeros((per_device,), jnp.int32)
        .at[jnp.where(owned, local_block, per_device).reshape(-1)]
        .set(sender_grid.reshape(-1), mode="drop")
    )
    placed = jnp.take(incoming, where_from, axis=1)
    levels = placed.reshape(2, length, height, breadth)
    wavelet_row = wavelet[0]
    receivers = receiver_cell[0]
    traces = residual[0]
    horizon = wavelet_row.shape[0]
    fields = [levels[0], levels[1]]
    adjoints = [None] * (horizon + 2)
    adjoints[horizon + 1] = adjoint_state[0, 0]
    adjoints[horizon] = adjoint_state[0, 1]
    for moment in range(1, horizon + 1):
        fields.append(
            advance(
                fields[-2],
                extend(fields[-1]),
                courant,
                wavelet_row[moment - 1 : moment],
                source_cell,
                first_row,
            )
        )
    for moment in range(horizon, 0, -1):
        weighted = extend(courant * adjoints[moment])
        adjoints[moment - 1] = retreat(
            adjoints[moment + 1],
            adjoints[moment],
            weighted,
            traces[moment - 1],
            receivers,
            first_row,
        )
    partial_value = jnp.zeros((length, height, breadth), jnp.float32)
    for moment in range(1, horizon + 1):
        partial_value = partial_value + adjoints[moment] * (
            fields[moment + 1] - 2.0 * fields[moment] + fields[moment - 1]
        )
    slab_rows = partial_value.reshape(length * height, breadth)
    check_part = jnp.sum(slab_rows[check_rows[0]], axis=1)
    stacked = jnp.concatenate([partial_value, check_part[None]], axis=0)
    shares = lax.psum_scatter(stacked, "shot", scatter_dimension=1, tiled=True)
    grad_share = shares[:length]
    check_share = shares[length]
    adjoint_carry = jnp.stack([adjoints[1], adjoints[0]])[None]
    return (grad_share, adjoint_carry, check_share[None])


def solution(mesh):
    in_specs = (
        P("space", None, None),
        P("shot", None, "space", None, None),
        P("shot", None),
        P("shot", None, "space", None, None),
        P("shot", None),
        P("shot"),
        P("shot", None),
        P("shot", None, None),
        P("space", None, None),
    )
    out_specs = (
        P("space", "shot", None),
        P("shot", None, "space", None, None),
        P("space", "shot", None),
    )
    return jax.shard_map(body, mesh=mesh, in_specs=in_specs, out_specs=out_specs, check_vma=False)
```

```python
import jax
import jax.numpy as jnp
from jax import lax
from jax.sharding import PartitionSpec as P

STENCIL = (-205.0 / 72.0, 8.0 / 5.0, -1.0 / 5.0, 8.0 / 315.0, -1.0 / 560.0)


def padded_2(array, sides, width):
    for axis, dim in sides:
        devices, length = (lax.axis_size(axis), array.shape[dim])
        up = [(i, (i + 1) % devices) for i in range(devices - 1)]
        down = [(j, i) for i, j in up]
        last = lax.slice_in_dim(array, length - width, length, axis=dim)
        initial = lax.slice_in_dim(array, 0, width, axis=dim)
        before = lax.ppermute(last, axis, up)
        after = lax.ppermute(initial, axis, down)
        array = jnp.concatenate([before, array, after], axis=dim)
    return array


def laplace(field):
    length = field.shape[0] - 8
    height = field.shape[1]
    breadth = field.shape[2]
    padded = jnp.pad(field, ((0, 0), (4, 4), (4, 4)))
    summed = 3.0 * STENCIL[0] * padded[4 : 4 + length, 4 : 4 + height, 4 : 4 + breadth]
    for offset in range(1, 5):
        summed = summed + STENCIL[offset] * (
            padded[4 + offset : 4 + offset + length, 4 : 4 + height, 4 : 4 + breadth]
            + padded[4 - offset : 4 - offset + length, 4 : 4 + height, 4 : 4 + breadth]
        )
    for offset in range(1, 5):
        summed = summed + STENCIL[offset] * (
            padded[4 : 4 + length, 4 + offset : 4 + offset + height, 4 : 4 + breadth]
            + padded[4 : 4 + length, 4 - offset : 4 - offset + height, 4 : 4 + breadth]
        )
    for offset in range(1, 5):
        summed = summed + STENCIL[offset] * (
            padded[4 : 4 + length, 4 : 4 + height, 4 + offset : 4 + offset + breadth]
            + padded[4 : 4 + length, 4 : 4 + height, 4 - offset : 4 - offset + breadth]
        )
    return summed


def inject(field, cell_index, values, first_row):
    plane_cells = field.shape[1] * field.shape[2]
    local_cell = cell_index - first_row * plane_cells
    inside = (local_cell >= 0) & (local_cell < field.shape[0] * plane_cells)
    target = jnp.where(inside, local_cell, field.shape[0] * plane_cells)
    flattened = field.reshape(-1).at[target].add(values, mode="drop")
    return flattened.reshape(field.shape)


def inject_dense(field, cell_index, values, first_row):
    plane_cells = field.shape[1] * field.shape[2]
    local_cell = cell_index[0] - first_row * plane_cells
    cells = (
        lax.broadcasted_iota(jnp.int32, field.shape, 0) * plane_cells
        + lax.broadcasted_iota(jnp.int32, field.shape, 1) * field.shape[2]
        + lax.broadcasted_iota(jnp.int32, field.shape, 2)
    )
    return field + jnp.where(cells == local_cell, values[0], 0.0)


def advance(before, current_ext, courant, wave_value, source, first_row):
    following = 2.0 * current_ext[4:-4] - before + courant * laplace(current_ext)
    return inject_dense(following, source, wave_value, first_row)


def retreat(following, current, weighted_ext, values, cell_index, first_row):
    earlier = 2.0 * current - following + laplace(weighted_ext)
    return inject(earlier, cell_index, values, first_row)


def extend(field):
    return padded_2(field, (("space", 0),), 4)


def body(
    courant,
    checkpoint,
    block_target,
    adjoint_state,
    wavelet,
    source_cell,
    receiver_cell,
    residual,
    check_rows,
):
    devices = lax.axis_size("space")
    position = lax.axis_index("space")
    length, height, breadth = courant.shape
    first_row = position * length
    per_device = checkpoint.shape[2]
    block_rows = checkpoint.shape[3]
    capacity = per_device // 4
    targets = block_target[0]
    payload = checkpoint[0]
    peers = targets // per_device
    lanes = jnp.arange(devices, dtype=jnp.int32)
    peer_grid = peers.reshape(devices, per_device)
    own_peers = lax.dynamic_index_in_dim(peer_grid, position, 0, keepdims=False)
    own_matches = (own_peers[:, None] == lanes[None, :]).astype(jnp.int32)
    own_ranks = jnp.sum((jnp.cumsum(own_matches, axis=0) - own_matches) * own_matches, axis=1)
    slot_of = own_peers * capacity + own_ranks
    source_of = (
        jnp.full((devices * capacity,), per_device, jnp.int32)
        .at[slot_of]
        .set(jnp.arange(per_device, dtype=jnp.int32))
    )
    by_block = jnp.transpose(payload, (1, 0, 2, 3))
    outgoing = jnp.take(by_block, source_of, axis=0, mode="fill", fill_value=0.0)
    outgoing = outgoing.reshape(devices, capacity, 2, block_rows, breadth)
    incoming = lax.all_to_all(outgoing, "space", split_axis=0, concat_axis=0, tiled=True)
    incoming = incoming.reshape(devices * capacity, 2, block_rows, breadth)
    matches = (peers[:, None] == lanes[None, :]).astype(jnp.int32)
    grouped = matches.reshape(devices, per_device, devices)
    ranking = jnp.sum((jnp.cumsum(grouped, axis=1) - grouped) * grouped, axis=2)
    sender_grid = lanes[:, None] * capacity + ranking
    owned = peer_grid == position
    local_block = (targets % per_device).reshape(devices, per_device)
    where_from = (
        jnp.zeros((per_device,), jnp.int32)
        .at[jnp.where(owned, local_block, per_device).reshape(-1)]
        .set(sender_grid.reshape(-1), mode="drop")
    )
    placed = jnp.transpose(jnp.take(incoming, where_from, axis=0), (1, 0, 2, 3))
    levels = placed.reshape(2, length, height, breadth)
    wavelet_row = wavelet[0]
    receivers = receiver_cell[0]
    traces = residual[0]
    horizon = wavelet_row.shape[0]
    fields = [levels[0], levels[1]]
    adjoints = [None] * (horizon + 2)
    adjoints[horizon + 1] = adjoint_state[0, 0]
    adjoints[horizon] = adjoint_state[0, 1]
    for moment in range(1, horizon + 1):
        fields.append(
            advance(
                fields[-2],
                extend(fields[-1]),
                courant,
                wavelet_row[moment - 1 : moment],
                source_cell,
                first_row,
            )
        )
    for moment in range(horizon, 0, -1):
        weighted = extend(courant * adjoints[moment])
        adjoints[moment - 1] = retreat(
            adjoints[moment + 1],
            adjoints[moment],
            weighted,
            traces[moment - 1],
            receivers,
            first_row,
        )
    partial_value = jnp.zeros((length, height, breadth), jnp.float32)
    for moment in range(1, horizon + 1):
        partial_value = partial_value + adjoints[moment] * (
            fields[moment + 1] - 2.0 * fields[moment] + fields[moment - 1]
        )
    slab_rows = partial_value.reshape(length * height, breadth)
    check_part = jnp.sum(slab_rows[check_rows[0]], axis=1)
    stacked = jnp.concatenate([partial_value, check_part[None]], axis=0)
    shot_devices = lax.axis_size("shot")
    pieces = stacked.reshape(length + 1, shot_devices, height // shot_devices, breadth)
    pieces = jnp.transpose(pieces, (1, 0, 2, 3))
    gathered = lax.all_to_all(pieces, "shot", split_axis=0, concat_axis=0, tiled=True)
    shares = jnp.sum(gathered, axis=0)
    grad_share = shares[:length]
    check_share = shares[length]
    adjoint_carry = jnp.stack([adjoints[1], adjoints[0]])[None]
    return (grad_share, adjoint_carry, check_share[None])


def solution(mesh):
    in_specs = (
        P("space", None, None),
        P("shot", None, "space", None, None),
        P("shot", None),
        P("shot", None, "space", None, None),
        P("shot", None),
        P("shot"),
        P("shot", None),
        P("shot", None, None),
        P("space", None, None),
    )
    out_specs = (
        P("space", "shot", None),
        P("shot", None, "space", None, None),
        P("space", "shot", None),
    )
    return jax.shard_map(body, mesh=mesh, in_specs=in_specs, out_specs=out_specs, check_vma=False)
```

```python
import jax
import jax.numpy as jnp
from jax import lax
from jax.sharding import PartitionSpec as P

STENCIL = (-205.0 / 72.0, 8.0 / 5.0, -1.0 / 5.0, 8.0 / 315.0, -1.0 / 560.0)


def padded_2(array, sides, width):
    for axis, dim in sides:
        devices, length = (lax.axis_size(axis), array.shape[dim])
        up = [(i, (i + 1) % devices) for i in range(devices - 1)]
        down = [(j, i) for i, j in up]
        last = lax.slice_in_dim(array, length - width, length, axis=dim)
        initial = lax.slice_in_dim(array, 0, width, axis=dim)
        before = lax.ppermute(last, axis, up)
        after = lax.ppermute(initial, axis, down)
        array = jnp.concatenate([before, array, after], axis=dim)
    return array


def laplace(field):
    length = field.shape[0] - 8
    height = field.shape[1]
    breadth = field.shape[2]
    padded = jnp.pad(field, ((0, 0), (4, 4), (4, 4)))
    summed = 3.0 * STENCIL[0] * padded[4 : 4 + length, 4 : 4 + height, 4 : 4 + breadth]
    for offset in range(1, 5):
        summed = summed + STENCIL[offset] * (
            padded[4 + offset : 4 + offset + length, 4 : 4 + height, 4 : 4 + breadth]
            + padded[4 - offset : 4 - offset + length, 4 : 4 + height, 4 : 4 + breadth]
        )
    for offset in range(1, 5):
        summed = summed + STENCIL[offset] * (
            padded[4 : 4 + length, 4 + offset : 4 + offset + height, 4 : 4 + breadth]
            + padded[4 : 4 + length, 4 - offset : 4 - offset + height, 4 : 4 + breadth]
        )
    for offset in range(1, 5):
        summed = summed + STENCIL[offset] * (
            padded[4 : 4 + length, 4 : 4 + height, 4 + offset : 4 + offset + breadth]
            + padded[4 : 4 + length, 4 : 4 + height, 4 - offset : 4 - offset + breadth]
        )
    return summed


def inject(field, cell_index, values, first_row):
    plane_cells = field.shape[1] * field.shape[2]
    local_cell = cell_index - first_row * plane_cells
    inside = (local_cell >= 0) & (local_cell < field.shape[0] * plane_cells)
    target = jnp.where(inside, local_cell, field.shape[0] * plane_cells)
    flattened = field.reshape(-1).at[target].add(values, mode="drop")
    return flattened.reshape(field.shape)


def inject_dense(field, cell_index, values, first_row):
    plane_cells = field.shape[1] * field.shape[2]
    local_cell = cell_index[0] - first_row * plane_cells
    cells = (
        lax.broadcasted_iota(jnp.int32, field.shape, 0) * plane_cells
        + lax.broadcasted_iota(jnp.int32, field.shape, 1) * field.shape[2]
        + lax.broadcasted_iota(jnp.int32, field.shape, 2)
    )
    return field + jnp.where(cells == local_cell, values[0], 0.0)


def advance(before, current_ext, courant, wave_value, source, first_row):
    following = 2.0 * current_ext[4:-4] - before + courant * laplace(current_ext)
    return inject_dense(following, source, wave_value, first_row)


def retreat(following, current, weighted_ext, values, cell_index, first_row):
    earlier = 2.0 * current - following + laplace(weighted_ext)
    return inject(earlier, cell_index, values, first_row)


def extend(field):
    return padded_2(field, (("space", 0),), 4)


def extend_many(fields, width=4):
    devices = lax.axis_size("space")
    up = [(i, (i + 1) % devices) for i in range(devices - 1)]
    down = [(j, i) for i, j in up]
    last = jnp.concatenate([f[f.shape[0] - width :] for f in fields], axis=0)
    initial = jnp.concatenate([f[:width] for f in fields], axis=0)
    before = lax.ppermute(last, "space", up)
    after = lax.ppermute(initial, "space", down)
    return [
        jnp.concatenate(
            [before[i * width : (i + 1) * width], f, after[i * width : (i + 1) * width]], axis=0
        )
        for i, f in enumerate(fields)
    ]


def body(
    courant,
    checkpoint,
    block_target,
    adjoint_state,
    wavelet,
    source_cell,
    receiver_cell,
    residual,
    check_rows,
):
    devices = lax.axis_size("space")
    position = lax.axis_index("space")
    length, height, breadth = courant.shape
    first_row = position * length
    per_device = checkpoint.shape[2]
    block_rows = checkpoint.shape[3]
    capacity = per_device // 4
    targets = block_target[0]
    payload = checkpoint[0]
    peers = targets // per_device
    lanes = jnp.arange(devices, dtype=jnp.int32)
    peer_grid = peers.reshape(devices, per_device)
    own_peers = lax.dynamic_index_in_dim(peer_grid, position, 0, keepdims=False)
    own_matches = (own_peers[:, None] == lanes[None, :]).astype(jnp.int32)
    own_ranks = jnp.sum((jnp.cumsum(own_matches, axis=0) - own_matches) * own_matches, axis=1)
    slot_of = own_peers * capacity + own_ranks
    source_of = (
        jnp.full((devices * capacity,), per_device, jnp.int32)
        .at[slot_of]
        .set(jnp.arange(per_device, dtype=jnp.int32))
    )
    by_block = jnp.transpose(payload, (1, 0, 2, 3))
    outgoing = jnp.take(by_block, source_of, axis=0, mode="fill", fill_value=0.0)
    outgoing = outgoing.reshape(devices, capacity, 2, block_rows, breadth)
    incoming = lax.all_to_all(outgoing, "space", split_axis=0, concat_axis=0, tiled=True)
    incoming = incoming.reshape(devices * capacity, 2, block_rows, breadth)
    matches = (peers[:, None] == lanes[None, :]).astype(jnp.int32)
    grouped = matches.reshape(devices, per_device, devices)
    ranking = jnp.sum((jnp.cumsum(grouped, axis=1) - grouped) * grouped, axis=2)
    sender_grid = lanes[:, None] * capacity + ranking
    owned = peer_grid == position
    local_block = (targets % per_device).reshape(devices, per_device)
    where_from = (
        jnp.zeros((per_device,), jnp.int32)
        .at[jnp.where(owned, local_block, per_device).reshape(-1)]
        .set(sender_grid.reshape(-1), mode="drop")
    )
    placed = jnp.transpose(jnp.take(incoming, where_from, axis=0), (1, 0, 2, 3))
    levels = placed.reshape(2, length, height, breadth)
    wavelet_row = wavelet[0]
    receivers = receiver_cell[0]
    traces = residual[0]
    horizon = wavelet_row.shape[0]
    fields = [levels[0], levels[1]]
    adjoints = [None] * (horizon + 2)
    adjoints[horizon + 1] = adjoint_state[0, 0]
    adjoints[horizon] = adjoint_state[0, 1]
    def forward_step(moment, current_ext):
        fields.append(
            advance(
                fields[-2],
                current_ext,
                courant,
                wavelet_row[moment - 1 : moment],
                source_cell,
                first_row,
            )
        )

    def adjoint_step(moment, weighted):
        adjoints[moment - 1] = retreat(
            adjoints[moment + 1],
            adjoints[moment],
            weighted,
            traces[moment - 1],
            receivers,
            first_row,
        )

    alone = horizon // 2
    for moment in range(horizon, horizon - alone, -1):
        adjoint_step(moment, extend(courant * adjoints[moment]))
    for moment in range(1, horizon + 1):
        back = horizon - alone + 1 - moment
        if back >= 1:
            current_ext, weighted = extend_many([fields[-1], courant * adjoints[back]])
            forward_step(moment, current_ext)
            adjoint_step(back, weighted)
        else:
            forward_step(moment, extend(fields[-1]))
    partial_value = jnp.zeros((length, height, breadth), jnp.float32)
    for moment in range(1, horizon + 1):
        partial_value = partial_value + adjoints[moment] * (
            fields[moment + 1] - 2.0 * fields[moment] + fields[moment - 1]
        )
    slab_rows = partial_value.reshape(length * height, breadth)
    row_ids = lax.broadcasted_iota(jnp.int32, (check_rows.shape[1], length * height), 1)
    counts = jnp.zeros((check_rows.shape[1], length * height), jnp.float32)
    for term in range(check_rows.shape[2]):
        counts = counts + (check_rows[0, :, term : term + 1] == row_ids).astype(jnp.float32)
    check_part = jnp.dot(counts, slab_rows, precision=lax.Precision.HIGHEST)
    stacked = jnp.concatenate([partial_value, check_part[None]], axis=0)
    shot_devices = lax.axis_size("shot")
    pieces = stacked.reshape(length + 1, shot_devices, height // shot_devices, breadth)
    pieces = jnp.transpose(pieces, (1, 0, 2, 3))
    gathered = lax.all_to_all(pieces, "shot", split_axis=0, concat_axis=0, tiled=True)
    shares = jnp.sum(gathered, axis=0)
    grad_share = shares[:length]
    check_share = shares[length]
    adjoint_carry = jnp.stack([adjoints[1], adjoints[0]])[None]
    return (grad_share, adjoint_carry, check_share[None])


def solution(mesh):
    in_specs = (
        P("space", None, None),
        P("shot", None, "space", None, None),
        P("shot", None),
        P("shot", None, "space", None, None),
        P("shot", None),
        P("shot"),
        P("shot", None),
        P("shot", None, None),
        P("space", None, None),
    )
    out_specs = (
        P("space", "shot", None),
        P("shot", None, "space", None, None),
        P("space", "shot", None),
    )
    return jax.shard_map(body, mesh=mesh, in_specs=in_specs, out_specs=out_specs, check_vma=False)
```

```python
import jax
import jax.numpy as jnp
from jax import lax
from jax.sharding import PartitionSpec as P

STENCIL = (-205.0 / 72.0, 8.0 / 5.0, -1.0 / 5.0, 8.0 / 315.0, -1.0 / 560.0)


def padded_2(array, sides, width):
    for axis, dim in sides:
        devices, length = (lax.axis_size(axis), array.shape[dim])
        up = [(i, (i + 1) % devices) for i in range(devices - 1)]
        down = [(j, i) for i, j in up]
        last = lax.slice_in_dim(array, length - width, length, axis=dim)
        initial = lax.slice_in_dim(array, 0, width, axis=dim)
        before = lax.ppermute(last, axis, up)
        after = lax.ppermute(initial, axis, down)
        array = jnp.concatenate([before, array, after], axis=dim)
    return array


def laplace(field):
    length = field.shape[0] - 8
    height = field.shape[1]
    breadth = field.shape[2]
    padded = jnp.pad(field, ((0, 0), (4, 4), (4, 4)))
    summed = 3.0 * STENCIL[0] * padded[4 : 4 + length, 4 : 4 + height, 4 : 4 + breadth]
    for offset in range(1, 5):
        summed = summed + STENCIL[offset] * (
            padded[4 + offset : 4 + offset + length, 4 : 4 + height, 4 : 4 + breadth]
            + padded[4 - offset : 4 - offset + length, 4 : 4 + height, 4 : 4 + breadth]
        )
    for offset in range(1, 5):
        summed = summed + STENCIL[offset] * (
            padded[4 : 4 + length, 4 + offset : 4 + offset + height, 4 : 4 + breadth]
            + padded[4 : 4 + length, 4 - offset : 4 - offset + height, 4 : 4 + breadth]
        )
    for offset in range(1, 5):
        summed = summed + STENCIL[offset] * (
            padded[4 : 4 + length, 4 : 4 + height, 4 + offset : 4 + offset + breadth]
            + padded[4 : 4 + length, 4 : 4 + height, 4 - offset : 4 - offset + breadth]
        )
    return summed


def inject(field, cell_index, values, first_row):
    plane_cells = field.shape[1] * field.shape[2]
    local_cell = cell_index - first_row * plane_cells
    inside = (local_cell >= 0) & (local_cell < field.shape[0] * plane_cells)
    target = jnp.where(inside, local_cell, field.shape[0] * plane_cells)
    flattened = field.reshape(-1).at[target].add(values, mode="drop")
    return flattened.reshape(field.shape)


def inject_dense(field, cell_index, values, first_row):
    plane_cells = field.shape[1] * field.shape[2]
    local_cell = cell_index[0] - first_row * plane_cells
    cells = (
        lax.broadcasted_iota(jnp.int32, field.shape, 0) * plane_cells
        + lax.broadcasted_iota(jnp.int32, field.shape, 1) * field.shape[2]
        + lax.broadcasted_iota(jnp.int32, field.shape, 2)
    )
    return field + jnp.where(cells == local_cell, values[0], 0.0)


def advance(before, current_ext, courant, wave_value, source, first_row):
    following = 2.0 * current_ext[4:-4] - before + courant * laplace(current_ext)
    return inject_dense(following, source, wave_value, first_row)


def retreat(following, current, weighted_ext, injected):
    return 2.0 * current - following + laplace(weighted_ext) + injected


def extend(field):
    return padded_2(field, (("space", 0),), 4)


def body(
    courant,
    checkpoint,
    block_target,
    adjoint_state,
    wavelet,
    source_cell,
    receiver_cell,
    residual,
    check_rows,
):
    devices = lax.axis_size("space")
    position = lax.axis_index("space")
    length, height, breadth = courant.shape
    first_row = position * length
    per_device = checkpoint.shape[2]
    block_rows = checkpoint.shape[3]
    capacity = per_device // 4
    targets = block_target[0]
    payload = checkpoint[0]
    peers = targets // per_device
    lanes = jnp.arange(devices, dtype=jnp.int32)
    peer_grid = peers.reshape(devices, per_device)
    own_peers = lax.dynamic_index_in_dim(peer_grid, position, 0, keepdims=False)
    own_matches = (own_peers[:, None] == lanes[None, :]).astype(jnp.int32)
    own_ranks = jnp.sum((jnp.cumsum(own_matches, axis=0) - own_matches) * own_matches, axis=1)
    slot_of = own_peers * capacity + own_ranks
    source_of = (
        jnp.full((devices * capacity,), per_device, jnp.int32)
        .at[slot_of]
        .set(jnp.arange(per_device, dtype=jnp.int32))
    )
    by_block = jnp.transpose(payload, (1, 0, 2, 3))
    by_block = jnp.concatenate([by_block, jnp.zeros_like(by_block[:1])], axis=0)
    outgoing = jnp.take(by_block, source_of, axis=0, mode="clip")
    outgoing = outgoing.reshape(devices, capacity, 2, block_rows, breadth)
    incoming = lax.all_to_all(outgoing, "space", split_axis=0, concat_axis=0, tiled=True)
    incoming = incoming.reshape(devices * capacity, 2, block_rows, breadth)
    matches = (peers[:, None] == lanes[None, :]).astype(jnp.int32)
    grouped = matches.reshape(devices, per_device, devices)
    ranking = jnp.sum((jnp.cumsum(grouped, axis=1) - grouped) * grouped, axis=2)
    sender_grid = lanes[:, None] * capacity + ranking
    owned = peer_grid == position
    local_block = (targets % per_device).reshape(devices, per_device)
    where_from = (
        jnp.zeros((per_device,), jnp.int32)
        .at[jnp.where(owned, local_block, per_device).reshape(-1)]
        .set(sender_grid.reshape(-1), mode="drop")
    )
    placed = jnp.transpose(jnp.take(incoming, where_from, axis=0), (1, 0, 2, 3))
    levels = placed.reshape(2, length, height, breadth)
    wavelet_row = wavelet[0]
    receivers = receiver_cell[0]
    traces = residual[0]
    horizon = wavelet_row.shape[0]
    fields = [levels[0], levels[1]]
    adjoints = [None] * (horizon + 2)
    adjoints[horizon + 1] = adjoint_state[0, 0]
    adjoints[horizon] = adjoint_state[0, 1]
    for moment in range(1, horizon + 1):
        fields.append(
            advance(
                fields[-2],
                extend(fields[-1]),
                courant,
                wavelet_row[moment - 1 : moment],
                source_cell,
                first_row,
            )
        )
    cells = length * height * breadth
    local_cells = receivers - first_row * height * breadth
    inside = (local_cells >= 0) & (local_cells < cells)
    steps = lax.broadcasted_iota(jnp.int32, traces.shape, 0)
    spots = jnp.where(inside[None, :], local_cells[None, :], cells)
    injections = (
        jnp.zeros((horizon, cells + 1), jnp.float32)
        .at[steps, jnp.broadcast_to(spots, traces.shape)]
        .add(traces, mode="drop")
    )
    for moment in range(horizon, 0, -1):
        weighted = extend(courant * adjoints[moment])
        adjoints[moment - 1] = retreat(
            adjoints[moment + 1],
            adjoints[moment],
            weighted,
            injections[moment - 1, :cells].reshape(length, height, breadth),
        )
    partial_value = jnp.zeros((length, height, breadth), jnp.float32)
    for moment in range(1, horizon + 1):
        partial_value = partial_value + adjoints[moment] * (
            fields[moment + 1] - 2.0 * fields[moment] + fields[moment - 1]
        )
    slab_rows = partial_value.reshape(length * height, breadth)
    row_ids = lax.broadcasted_iota(jnp.int32, (1, 1, length * height), 2)
    counts = jnp.sum((check_rows[0][:, :, None] == row_ids).astype(jnp.float32), axis=1)
    check_part = jnp.dot(counts, slab_rows, precision=lax.Precision.HIGHEST)
    stacked = jnp.concatenate([partial_value, check_part[None]], axis=0)
    shot_devices = lax.axis_size("shot")
    pieces = stacked.reshape(length + 1, shot_devices, height // shot_devices, breadth)
    pieces = jnp.transpose(pieces, (1, 0, 2, 3))
    gathered = lax.all_to_all(pieces, "shot", split_axis=0, concat_axis=0, tiled=True)
    grad_share = jnp.sum(gathered[:, :length], axis=0)
    check_share = jnp.sum(gathered[:, length], axis=0)
    adjoint_carry = jnp.stack([adjoints[1], adjoints[0]])[None]
    return (grad_share, adjoint_carry, check_share[None])


def solution(mesh):
    in_specs = (
        P("space", None, None),
        P("shot", None, "space", None, None),
        P("shot", None),
        P("shot", None, "space", None, None),
        P("shot", None),
        P("shot"),
        P("shot", None),
        P("shot", None, None),
        P("space", None, None),
    )
    out_specs = (
        P("space", "shot", None),
        P("shot", None, "space", None, None),
        P("space", "shot", None),
    )
    return jax.shard_map(body, mesh=mesh, in_specs=in_specs, out_specs=out_specs, check_vma=False)
```

```python
import jax
import jax.numpy as jnp
from jax import lax
from jax.sharding import PartitionSpec as P

STENCIL = (-205.0 / 72.0, 8.0 / 5.0, -1.0 / 5.0, 8.0 / 315.0, -1.0 / 560.0)


def padded_2(array, sides, width):
    for axis, dim in sides:
        devices, length = (lax.axis_size(axis), array.shape[dim])
        up = [(i, (i + 1) % devices) for i in range(devices - 1)]
        down = [(j, i) for i, j in up]
        last = lax.slice_in_dim(array, length - width, length, axis=dim)
        initial = lax.slice_in_dim(array, 0, width, axis=dim)
        before = lax.ppermute(last, axis, up)
        after = lax.ppermute(initial, axis, down)
        array = jnp.concatenate([before, array, after], axis=dim)
    return array


def laplace(field):
    length = field.shape[0] - 8
    height = field.shape[1]
    breadth = field.shape[2]
    padded = jnp.pad(field, ((0, 0), (4, 4), (4, 4)))
    summed = 3.0 * STENCIL[0] * padded[4 : 4 + length, 4 : 4 + height, 4 : 4 + breadth]
    for offset in range(1, 5):
        summed = summed + STENCIL[offset] * (
            padded[4 + offset : 4 + offset + length, 4 : 4 + height, 4 : 4 + breadth]
            + padded[4 - offset : 4 - offset + length, 4 : 4 + height, 4 : 4 + breadth]
        )
    for offset in range(1, 5):
        summed = summed + STENCIL[offset] * (
            padded[4 : 4 + length, 4 + offset : 4 + offset + height, 4 : 4 + breadth]
            + padded[4 : 4 + length, 4 - offset : 4 - offset + height, 4 : 4 + breadth]
        )
    for offset in range(1, 5):
        summed = summed + STENCIL[offset] * (
            padded[4 : 4 + length, 4 : 4 + height, 4 + offset : 4 + offset + breadth]
            + padded[4 : 4 + length, 4 : 4 + height, 4 - offset : 4 - offset + breadth]
        )
    return summed


def inject(field, cell_index, values, first_row):
    plane_cells = field.shape[1] * field.shape[2]
    local_cell = cell_index - first_row * plane_cells
    inside = (local_cell >= 0) & (local_cell < field.shape[0] * plane_cells)
    target = jnp.where(inside, local_cell, field.shape[0] * plane_cells)
    flattened = field.reshape(-1).at[target].add(values, mode="drop")
    return flattened.reshape(field.shape)


def inject_dense(field, cell_index, values, first_row):
    plane_cells = field.shape[1] * field.shape[2]
    local_cell = cell_index[0] - first_row * plane_cells
    cells = (
        lax.broadcasted_iota(jnp.int32, field.shape, 0) * plane_cells
        + lax.broadcasted_iota(jnp.int32, field.shape, 1) * field.shape[2]
        + lax.broadcasted_iota(jnp.int32, field.shape, 2)
    )
    return field + jnp.where(cells == local_cell, values[0], 0.0)


def advance(before, current_ext, courant, wave_value, source, first_row):
    following = 2.0 * current_ext[4:-4] - before + courant * laplace(current_ext)
    return inject_dense(following, source, wave_value, first_row)


def retreat(following, current, weighted_ext, injected):
    return 2.0 * current - following + laplace(weighted_ext) + injected


def extend(field):
    return padded_2(field, (("space", 0),), 4)


def body(
    courant,
    checkpoint,
    block_target,
    adjoint_state,
    wavelet,
    source_cell,
    receiver_cell,
    residual,
    check_rows,
):
    devices = lax.axis_size("space")
    position = lax.axis_index("space")
    length, height, breadth = courant.shape
    first_row = position * length
    per_device = checkpoint.shape[2]
    block_rows = checkpoint.shape[3]
    capacity = per_device // 4
    targets = block_target[0]
    payload = checkpoint[0]
    peers = targets // per_device
    lanes = jnp.arange(devices, dtype=jnp.int32)
    peer_grid = peers.reshape(devices, per_device)
    own_peers = lax.dynamic_index_in_dim(peer_grid, position, 0, keepdims=False)
    own_matches = (own_peers[:, None] == lanes[None, :]).astype(jnp.int32)
    own_ranks = jnp.sum((jnp.cumsum(own_matches, axis=0) - own_matches) * own_matches, axis=1)
    slot_of = own_peers * capacity + own_ranks
    source_of = (
        jnp.full((devices * capacity,), per_device, jnp.int32)
        .at[slot_of]
        .set(jnp.arange(per_device, dtype=jnp.int32))
    )
    by_block = jnp.transpose(payload, (1, 0, 2, 3))
    by_block = jnp.concatenate([by_block, jnp.zeros_like(by_block[:1])], axis=0)
    outgoing = jnp.take(by_block, source_of, axis=0, mode="clip")
    outgoing = outgoing.reshape(devices, capacity, 2, block_rows, breadth)
    incoming = [
        lax.all_to_all(outgoing[:, :, level], "space", split_axis=0, concat_axis=0, tiled=True)
        for level in (1, 0)
    ]
    incoming = [part.reshape(devices * capacity, block_rows, breadth) for part in incoming[::-1]]
    matches = (peers[:, None] == lanes[None, :]).astype(jnp.int32)
    grouped = matches.reshape(devices, per_device, devices)
    ranking = jnp.sum((jnp.cumsum(grouped, axis=1) - grouped) * grouped, axis=2)
    sender_grid = lanes[:, None] * capacity + ranking
    owned = peer_grid == position
    local_block = (targets % per_device).reshape(devices, per_device)
    where_from = (
        jnp.zeros((per_device,), jnp.int32)
        .at[jnp.where(owned, local_block, per_device).reshape(-1)]
        .set(sender_grid.reshape(-1), mode="drop")
    )
    levels = [jnp.take(part, where_from, axis=0).reshape(length, height, breadth) for part in incoming]
    wavelet_row = wavelet[0]
    receivers = receiver_cell[0]
    traces = residual[0]
    horizon = wavelet_row.shape[0]
    fields = [levels[0], levels[1]]
    adjoints = [None] * (horizon + 2)
    adjoints[horizon + 1] = adjoint_state[0, 0]
    adjoints[horizon] = adjoint_state[0, 1]
    for moment in range(1, horizon + 1):
        fields.append(
            advance(
                fields[-2],
                extend(fields[-1]),
                courant,
                wavelet_row[moment - 1 : moment],
                source_cell,
                first_row,
            )
        )
    cells = length * height * breadth
    local_cells = receivers - first_row * height * breadth
    inside = (local_cells >= 0) & (local_cells < cells)
    steps = lax.broadcasted_iota(jnp.int32, traces.shape, 0)
    spots = jnp.where(inside[None, :], local_cells[None, :], cells)
    injections = (
        jnp.zeros((horizon, cells + 1), jnp.float32)
        .at[steps, jnp.broadcast_to(spots, traces.shape)]
        .add(traces, mode="drop")
    )
    for moment in range(horizon, 0, -1):
        weighted = extend(courant * adjoints[moment])
        adjoints[moment - 1] = retreat(
            adjoints[moment + 1],
            adjoints[moment],
            weighted,
            injections[moment - 1, :cells].reshape(length, height, breadth),
        )
    partial_value = jnp.zeros((length, height, breadth), jnp.float32)
    for moment in range(1, horizon + 1):
        partial_value = partial_value + adjoints[moment] * (
            fields[moment + 1] - 2.0 * fields[moment] + fields[moment - 1]
        )
    slab_rows = partial_value.reshape(length * height, breadth)
    row_ids = lax.broadcasted_iota(jnp.int32, (1, 1, length * height), 2)
    counts = jnp.sum((check_rows[0][:, :, None] == row_ids).astype(jnp.float32), axis=1)
    check_part = jnp.dot(counts, slab_rows, precision=lax.Precision.HIGHEST)
    stacked = jnp.concatenate([partial_value, check_part[None]], axis=0)
    shot_devices = lax.axis_size("shot")
    pieces = stacked.reshape(length + 1, shot_devices, height // shot_devices, breadth)
    pieces = jnp.transpose(pieces, (1, 0, 2, 3))
    gathered = lax.all_to_all(pieces, "shot", split_axis=0, concat_axis=0, tiled=True)
    grad_share = jnp.sum(gathered[:, :length], axis=0)
    check_share = jnp.sum(gathered[:, length], axis=0)
    adjoint_carry = jnp.stack([adjoints[1], adjoints[0]])[None]
    return (grad_share, adjoint_carry, check_share[None])


def solution(mesh):
    in_specs = (
        P("space", None, None),
        P("shot", None, "space", None, None),
        P("shot", None),
        P("shot", None, "space", None, None),
        P("shot", None),
        P("shot"),
        P("shot", None),
        P("shot", None, None),
        P("space", None, None),
    )
    out_specs = (
        P("space", "shot", None),
        P("shot", None, "space", None, None),
        P("space", "shot", None),
    )
    return jax.shard_map(body, mesh=mesh, in_specs=in_specs, out_specs=out_specs, check_vma=False)
```

```python
import jax
import jax.numpy as jnp
from jax import lax
from jax.sharding import PartitionSpec as P

STENCIL = (-205.0 / 72.0, 8.0 / 5.0, -1.0 / 5.0, 8.0 / 315.0, -1.0 / 560.0)


def padded_2(array, sides, width):
    for axis, dim in sides:
        devices, length = (lax.axis_size(axis), array.shape[dim])
        up = [(i, (i + 1) % devices) for i in range(devices - 1)]
        down = [(j, i) for i, j in up]
        last = lax.slice_in_dim(array, length - width, length, axis=dim)
        initial = lax.slice_in_dim(array, 0, width, axis=dim)
        before = lax.ppermute(last, axis, up)
        after = lax.ppermute(initial, axis, down)
        array = jnp.concatenate([before, array, after], axis=dim)
    return array


def laplace(field):
    length = field.shape[0] - 8
    height = field.shape[1]
    breadth = field.shape[2]
    padded = jnp.pad(field, ((0, 0), (4, 4), (4, 4)))
    summed = 3.0 * STENCIL[0] * padded[4 : 4 + length, 4 : 4 + height, 4 : 4 + breadth]
    for offset in range(1, 5):
        summed = summed + STENCIL[offset] * (
            padded[4 + offset : 4 + offset + length, 4 : 4 + height, 4 : 4 + breadth]
            + padded[4 - offset : 4 - offset + length, 4 : 4 + height, 4 : 4 + breadth]
        )
    for offset in range(1, 5):
        summed = summed + STENCIL[offset] * (
            padded[4 : 4 + length, 4 + offset : 4 + offset + height, 4 : 4 + breadth]
            + padded[4 : 4 + length, 4 - offset : 4 - offset + height, 4 : 4 + breadth]
        )
    for offset in range(1, 5):
        summed = summed + STENCIL[offset] * (
            padded[4 : 4 + length, 4 : 4 + height, 4 + offset : 4 + offset + breadth]
            + padded[4 : 4 + length, 4 : 4 + height, 4 - offset : 4 - offset + breadth]
        )
    return summed


def inject(field, cell_index, values, first_row):
    plane_cells = field.shape[1] * field.shape[2]
    local_cell = cell_index - first_row * plane_cells
    inside = (local_cell >= 0) & (local_cell < field.shape[0] * plane_cells)
    target = jnp.where(inside, local_cell, field.shape[0] * plane_cells)
    flattened = field.reshape(-1).at[target].add(values, mode="drop")
    return flattened.reshape(field.shape)


def inject_dense(field, cell_index, values, first_row):
    plane_cells = field.shape[1] * field.shape[2]
    local_cell = cell_index[0] - first_row * plane_cells
    cells = (
        lax.broadcasted_iota(jnp.int32, field.shape, 0) * plane_cells
        + lax.broadcasted_iota(jnp.int32, field.shape, 1) * field.shape[2]
        + lax.broadcasted_iota(jnp.int32, field.shape, 2)
    )
    return field + jnp.where(cells == local_cell, values[0], 0.0)


def advance(before, current_ext, courant, wave_value, source, first_row):
    following = 2.0 * current_ext[4:-4] - before + courant * laplace(current_ext)
    return inject_dense(following, source, wave_value, first_row)


def retreat(following, current, weighted_ext, injected):
    return 2.0 * current - following + laplace(weighted_ext) + injected


def extend(field):
    return padded_2(field, (("space", 0),), 4)


def body(
    courant,
    checkpoint,
    block_target,
    adjoint_state,
    wavelet,
    source_cell,
    receiver_cell,
    residual,
    check_rows,
):
    devices = lax.axis_size("space")
    position = lax.axis_index("space")
    length, height, breadth = courant.shape
    first_row = position * length
    per_device = checkpoint.shape[2]
    block_rows = checkpoint.shape[3]
    capacity = per_device // 4
    targets = block_target[0]
    payload = checkpoint[0]
    peers = targets // per_device
    lanes = jnp.arange(devices, dtype=jnp.int32)
    peer_grid = peers.reshape(devices, per_device)
    own_peers = lax.dynamic_index_in_dim(peer_grid, position, 0, keepdims=False)
    own_matches = (own_peers[:, None] == lanes[None, :]).astype(jnp.int32)
    own_ranks = jnp.sum((jnp.cumsum(own_matches, axis=0) - own_matches) * own_matches, axis=1)
    slot_of = own_peers * capacity + own_ranks
    source_of = (
        jnp.full((devices * capacity,), per_device, jnp.int32)
        .at[slot_of]
        .set(jnp.arange(per_device, dtype=jnp.int32))
    )
    by_block = jnp.transpose(payload, (1, 0, 2, 3))
    by_block = jnp.concatenate([by_block, jnp.zeros_like(by_block[:1])], axis=0)
    outgoing = jnp.take(by_block, source_of, axis=0, mode="clip")
    outgoing = outgoing.reshape(devices, capacity, 2, block_rows, breadth)
    incoming = lax.all_to_all(outgoing, "space", split_axis=0, concat_axis=0, tiled=True)
    incoming = incoming.reshape(devices * capacity, 2, block_rows, breadth)
    matches = (peers[:, None] == lanes[None, :]).astype(jnp.int32)
    grouped = matches.reshape(devices, per_device, devices)
    ranking = jnp.sum((jnp.cumsum(grouped, axis=1) - grouped) * grouped, axis=2)
    sender_grid = lanes[:, None] * capacity + ranking
    owned = peer_grid == position
    local_block = (targets % per_device).reshape(devices, per_device)
    where_from = (
        jnp.zeros((per_device,), jnp.int32)
        .at[jnp.where(owned, local_block, per_device).reshape(-1)]
        .set(sender_grid.reshape(-1), mode="drop")
    )
    levels = [
        jnp.take(incoming[:, level], where_from, axis=0).reshape(length, height, breadth)
        for level in (0, 1)
    ]
    wavelet_row = wavelet[0]
    receivers = receiver_cell[0]
    traces = residual[0]
    horizon = wavelet_row.shape[0]
    fields = [levels[0], levels[1]]
    adjoints = [None] * (horizon + 2)
    adjoints[horizon + 1] = adjoint_state[0, 0]
    adjoints[horizon] = adjoint_state[0, 1]
    cells = length * height * breadth
    local_cells = receivers - first_row * height * breadth
    inside = (local_cells >= 0) & (local_cells < cells)
    steps = lax.broadcasted_iota(jnp.int32, traces.shape, 0)
    spots = jnp.where(inside[None, :], local_cells[None, :], cells)
    injections = (
        jnp.zeros((horizon, cells + 1), jnp.float32)
        .at[steps, jnp.broadcast_to(spots, traces.shape)]
        .add(traces, mode="drop")
    )

    def adjoint_step(moment, weighted):
        adjoints[moment - 1] = retreat(
            adjoints[moment + 1],
            adjoints[moment],
            weighted,
            injections[moment - 1, :cells].reshape(length, height, breadth),
        )

    for moment in range(horizon, 1, -1):
        adjoint_step(moment, extend(courant * adjoints[moment]))
    for moment in range(1, horizon + 1):
        fields.append(
            advance(
                fields[-2],
                extend(fields[-1]),
                courant,
                wavelet_row[moment - 1 : moment],
                source_cell,
                first_row,
            )
        )
    fields[-1], last_weighted = lax.optimization_barrier((fields[-1], courant * adjoints[1]))
    adjoint_step(1, extend(last_weighted))
    partial_value = jnp.zeros((length, height, breadth), jnp.float32)
    for moment in range(1, horizon + 1):
        partial_value = partial_value + adjoints[moment] * (
            fields[moment + 1] - 2.0 * fields[moment] + fields[moment - 1]
        )
    slab_rows = partial_value.reshape(length * height, breadth)
    row_ids = lax.broadcasted_iota(jnp.int32, (1, 1, length * height), 2)
    counts = jnp.sum((check_rows[0][:, :, None] == row_ids).astype(jnp.float32), axis=1)
    check_part = jnp.dot(counts, slab_rows, precision=lax.Precision.HIGHEST)
    stacked = jnp.concatenate([partial_value, check_part[None]], axis=0)
    shot_devices = lax.axis_size("shot")
    pieces = stacked.reshape(length + 1, shot_devices, height // shot_devices, breadth)
    pieces = jnp.transpose(pieces, (1, 0, 2, 3))
    gathered = lax.all_to_all(pieces, "shot", split_axis=0, concat_axis=0, tiled=True)
    grad_share = jnp.sum(gathered[:, :length], axis=0)
    check_share = jnp.sum(gathered[:, length], axis=0)
    adjoint_carry = jnp.stack([adjoints[1], adjoints[0]])[None]
    return (grad_share, adjoint_carry, check_share[None])


def solution(mesh):
    in_specs = (
        P("space", None, None),
        P("shot", None, "space", None, None),
        P("shot", None),
        P("shot", None, "space", None, None),
        P("shot", None),
        P("shot"),
        P("shot", None),
        P("shot", None, None),
        P("space", None, None),
    )
    out_specs = (
        P("space", "shot", None),
        P("shot", None, "space", None, None),
        P("space", "shot", None),
    )
    return jax.shard_map(body, mesh=mesh, in_specs=in_specs, out_specs=out_specs, check_vma=False)
```

```python
import jax
import jax.numpy as jnp
from jax import lax
from jax.sharding import PartitionSpec as P

STENCIL = (-205.0 / 72.0, 8.0 / 5.0, -1.0 / 5.0, 8.0 / 315.0, -1.0 / 560.0)


def padded_2(array, sides, width):
    for axis, dim in sides:
        devices, length = (lax.axis_size(axis), array.shape[dim])
        up = [(i, (i + 1) % devices) for i in range(devices - 1)]
        down = [(j, i) for i, j in up]
        last = lax.slice_in_dim(array, length - width, length, axis=dim)
        initial = lax.slice_in_dim(array, 0, width, axis=dim)
        before = lax.ppermute(last, axis, up)
        after = lax.ppermute(initial, axis, down)
        array = jnp.concatenate([before, array, after], axis=dim)
    return array


def laplace(field):
    length = field.shape[0] - 8
    height = field.shape[1]
    breadth = field.shape[2]
    padded = jnp.pad(field, ((0, 0), (4, 4), (4, 4)))
    summed = 3.0 * STENCIL[0] * padded[4 : 4 + length, 4 : 4 + height, 4 : 4 + breadth]
    for offset in range(1, 5):
        summed = summed + STENCIL[offset] * (
            padded[4 + offset : 4 + offset + length, 4 : 4 + height, 4 : 4 + breadth]
            + padded[4 - offset : 4 - offset + length, 4 : 4 + height, 4 : 4 + breadth]
        )
    for offset in range(1, 5):
        summed = summed + STENCIL[offset] * (
            padded[4 : 4 + length, 4 + offset : 4 + offset + height, 4 : 4 + breadth]
            + padded[4 : 4 + length, 4 - offset : 4 - offset + height, 4 : 4 + breadth]
        )
    for offset in range(1, 5):
        summed = summed + STENCIL[offset] * (
            padded[4 : 4 + length, 4 : 4 + height, 4 + offset : 4 + offset + breadth]
            + padded[4 : 4 + length, 4 : 4 + height, 4 - offset : 4 - offset + breadth]
        )
    return summed


def inject(field, cell_index, values, first_row):
    plane_cells = field.shape[1] * field.shape[2]
    local_cell = cell_index - first_row * plane_cells
    inside = (local_cell >= 0) & (local_cell < field.shape[0] * plane_cells)
    target = jnp.where(inside, local_cell, field.shape[0] * plane_cells)
    flattened = field.reshape(-1).at[target].add(values, mode="drop")
    return flattened.reshape(field.shape)


def inject_dense(field, cell_index, values, first_row):
    plane_cells = field.shape[1] * field.shape[2]
    local_cell = cell_index[0] - first_row * plane_cells
    cells = (
        lax.broadcasted_iota(jnp.int32, field.shape, 0) * plane_cells
        + lax.broadcasted_iota(jnp.int32, field.shape, 1) * field.shape[2]
        + lax.broadcasted_iota(jnp.int32, field.shape, 2)
    )
    return field + jnp.where(cells == local_cell, values[0], 0.0)


def advance(before, current_ext, courant, wave_value, source, first_row):
    following = 2.0 * current_ext[4:-4] - before + courant * laplace(current_ext)
    return inject_dense(following, source, wave_value, first_row)


def retreat(following, current, weighted_ext, injected):
    return 2.0 * current - following + laplace(weighted_ext) + injected


def extend(field):
    return padded_2(field, (("space", 0),), 4)


def body(
    courant,
    checkpoint,
    block_target,
    adjoint_state,
    wavelet,
    source_cell,
    receiver_cell,
    residual,
    check_rows,
):
    devices = lax.axis_size("space")
    position = lax.axis_index("space")
    length, height, breadth = courant.shape
    first_row = position * length
    per_device = checkpoint.shape[2]
    block_rows = checkpoint.shape[3]
    capacity = per_device // 4
    targets = block_target[0]
    payload = checkpoint[0]
    peers = targets // per_device
    lanes = jnp.arange(devices, dtype=jnp.int32)
    peer_grid = peers.reshape(devices, per_device)
    own_peers = lax.dynamic_index_in_dim(peer_grid, position, 0, keepdims=False)
    own_matches = (own_peers[:, None] == lanes[None, :]).astype(jnp.int32)
    own_ranks = jnp.sum((jnp.cumsum(own_matches, axis=0) - own_matches) * own_matches, axis=1)
    slot_of = own_peers * capacity + own_ranks
    source_of = (
        jnp.full((devices * capacity,), per_device, jnp.int32)
        .at[slot_of]
        .set(jnp.arange(per_device, dtype=jnp.int32))
    )
    by_block = jnp.transpose(payload, (1, 0, 2, 3))
    outgoing = jnp.take(by_block, source_of, axis=0, mode="clip")
    outgoing = outgoing.reshape(devices, capacity, 2, block_rows, breadth)
    incoming = lax.all_to_all(outgoing, "space", split_axis=0, concat_axis=0, tiled=True)
    incoming = incoming.reshape(devices * capacity, 2, block_rows, breadth)
    matches = (peers[:, None] == lanes[None, :]).astype(jnp.int32)
    grouped = matches.reshape(devices, per_device, devices)
    ranking = jnp.sum((jnp.cumsum(grouped, axis=1) - grouped) * grouped, axis=2)
    sender_grid = lanes[:, None] * capacity + ranking
    owned = peer_grid == position
    local_block = (targets % per_device).reshape(devices, per_device)
    where_from = (
        jnp.zeros((per_device,), jnp.int32)
        .at[jnp.where(owned, local_block, per_device).reshape(-1)]
        .set(sender_grid.reshape(-1), mode="drop")
    )
    placed = jnp.transpose(jnp.take(incoming, where_from, axis=0, mode="clip"), (1, 0, 2, 3))
    levels = placed.reshape(2, length, height, breadth)
    wavelet_row = wavelet[0]
    receivers = receiver_cell[0]
    traces = residual[0]
    horizon = wavelet_row.shape[0]
    fields = [levels[0], levels[1]]
    adjoints = [None] * (horizon + 2)
    adjoints[horizon + 1] = adjoint_state[0, 0]
    adjoints[horizon] = adjoint_state[0, 1]
    for moment in range(1, horizon + 1):
        fields.append(
            advance(
                fields[-2],
                extend(fields[-1]),
                courant,
                wavelet_row[moment - 1 : moment],
                source_cell,
                first_row,
            )
        )
    cells = length * height * breadth
    local_cells = receivers - first_row * height * breadth
    inside = (local_cells >= 0) & (local_cells < cells)
    steps = lax.broadcasted_iota(jnp.int32, traces.shape, 0)
    spots = jnp.where(inside[None, :], local_cells[None, :], cells)
    injections = (
        jnp.zeros((horizon, cells + 1), jnp.float32)
        .at[steps, jnp.broadcast_to(spots, traces.shape)]
        .add(traces, mode="drop")
    )
    for moment in range(horizon, 0, -1):
        weighted = extend(courant * adjoints[moment])
        adjoints[moment - 1] = retreat(
            adjoints[moment + 1],
            adjoints[moment],
            weighted,
            injections[moment - 1, :cells].reshape(length, height, breadth),
        )
    partial_value = jnp.zeros((length, height, breadth), jnp.float32)
    for moment in range(1, horizon + 1):
        partial_value = partial_value + adjoints[moment] * (
            fields[moment + 1] - 2.0 * fields[moment] + fields[moment - 1]
        )
    slab_rows = partial_value.reshape(length * height, breadth)
    row_ids = lax.broadcasted_iota(jnp.int32, (1, 1, length * height), 2)
    counts = jnp.sum((check_rows[0][:, :, None] == row_ids).astype(jnp.float32), axis=1)
    check_part = jnp.dot(counts, slab_rows, precision=lax.Precision.HIGHEST)
    stacked = jnp.concatenate([partial_value, check_part[None]], axis=0)
    shot_devices = lax.axis_size("shot")
    pieces = stacked.reshape(length + 1, shot_devices, height // shot_devices, breadth)
    pieces = jnp.transpose(pieces, (1, 0, 2, 3))
    gathered = lax.all_to_all(pieces, "shot", split_axis=0, concat_axis=0, tiled=True)
    grad_share = jnp.sum(gathered[:, :length], axis=0)
    check_share = jnp.sum(gathered[:, length], axis=0)
    adjoint_carry = jnp.stack([adjoints[1], adjoints[0]])[None]
    return (grad_share, adjoint_carry, check_share[None])


def solution(mesh):
    in_specs = (
        P("space", None, None),
        P("shot", None, "space", None, None),
        P("shot", None),
        P("shot", None, "space", None, None),
        P("shot", None),
        P("shot"),
        P("shot", None),
        P("shot", None, None),
        P("space", None, None),
    )
    out_specs = (
        P("space", "shot", None),
        P("shot", None, "space", None, None),
        P("space", "shot", None),
    )
    return jax.shard_map(body, mesh=mesh, in_specs=in_specs, out_specs=out_specs, check_vma=False)
```

```python
import jax
import jax.numpy as jnp
from jax import lax
from jax.sharding import PartitionSpec as P

STENCIL = (-205.0 / 72.0, 8.0 / 5.0, -1.0 / 5.0, 8.0 / 315.0, -1.0 / 560.0)


def padded_2(array, sides, width):
    for axis, dim in sides:
        devices, length = (lax.axis_size(axis), array.shape[dim])
        up = [(i, (i + 1) % devices) for i in range(devices - 1)]
        down = [(j, i) for i, j in up]
        last = lax.slice_in_dim(array, length - width, length, axis=dim)
        initial = lax.slice_in_dim(array, 0, width, axis=dim)
        before = lax.ppermute(last, axis, up)
        after = lax.ppermute(initial, axis, down)
        array = jnp.concatenate([before, array, after], axis=dim)
    return array


def shifted(field, offset, axis):
    length = field.shape[axis]
    pad = [(0, 0)] * field.ndim
    if offset > 0:
        part = lax.slice_in_dim(field, offset, length, axis=axis)
        pad[axis] = (0, offset)
    else:
        part = lax.slice_in_dim(field, 0, length + offset, axis=axis)
        pad[axis] = (-offset, 0)
    return jnp.pad(part, pad)


def laplace(field):
    length = field.shape[0] - 8
    center = field[4 : 4 + length]
    summed = 3.0 * STENCIL[0] * center
    for offset in range(1, 5):
        summed = summed + STENCIL[offset] * (
            field[4 + offset : 4 + offset + length] + field[4 - offset : 4 - offset + length]
        )
    for axis in (1, 2):
        for offset in range(1, 5):
            summed = summed + STENCIL[offset] * (
                shifted(center, offset, axis) + shifted(center, -offset, axis)
            )
    return summed


def inject(field, cell_index, values, first_row):
    plane_cells = field.shape[1] * field.shape[2]
    local_cell = cell_index - first_row * plane_cells
    inside = (local_cell >= 0) & (local_cell < field.shape[0] * plane_cells)
    target = jnp.where(inside, local_cell, field.shape[0] * plane_cells)
    flattened = field.reshape(-1).at[target].add(values, mode="drop")
    return flattened.reshape(field.shape)


def inject_dense(field, cell_index, values, first_row):
    plane_cells = field.shape[1] * field.shape[2]
    local_cell = cell_index[0] - first_row * plane_cells
    cells = (
        lax.broadcasted_iota(jnp.int32, field.shape, 0) * plane_cells
        + lax.broadcasted_iota(jnp.int32, field.shape, 1) * field.shape[2]
        + lax.broadcasted_iota(jnp.int32, field.shape, 2)
    )
    return field + jnp.where(cells == local_cell, values[0], 0.0)


def advance(before, current_ext, courant, wave_value, source, first_row):
    following = 2.0 * current_ext[4:-4] - before + courant * laplace(current_ext)
    return inject_dense(following, source, wave_value, first_row)


def retreat(following, current, weighted_ext, injected):
    return 2.0 * current - following + laplace(weighted_ext) + injected


def extend(field):
    return padded_2(field, (("space", 0),), 4)


def body(
    courant,
    checkpoint,
    block_target,
    adjoint_state,
    wavelet,
    source_cell,
    receiver_cell,
    residual,
    check_rows,
):
    devices = lax.axis_size("space")
    position = lax.axis_index("space")
    length, height, breadth = courant.shape
    first_row = position * length
    per_device = checkpoint.shape[2]
    block_rows = checkpoint.shape[3]
    capacity = per_device // 4
    targets = block_target[0]
    payload = checkpoint[0]
    peers = targets // per_device
    lanes = jnp.arange(devices, dtype=jnp.int32)
    peer_grid = peers.reshape(devices, per_device)
    own_peers = lax.dynamic_index_in_dim(peer_grid, position, 0, keepdims=False)
    own_matches = (own_peers[:, None] == lanes[None, :]).astype(jnp.int32)
    own_ranks = jnp.sum((jnp.cumsum(own_matches, axis=0) - own_matches) * own_matches, axis=1)
    slot_of = own_peers * capacity + own_ranks
    source_of = (
        jnp.full((devices * capacity,), per_device, jnp.int32)
        .at[slot_of]
        .set(jnp.arange(per_device, dtype=jnp.int32))
    )
    by_block = jnp.transpose(payload, (1, 0, 2, 3))
    by_block = jnp.concatenate([by_block, jnp.zeros_like(by_block[:1])], axis=0)
    outgoing = jnp.take(by_block, source_of, axis=0, mode="clip")
    outgoing = outgoing.reshape(devices, capacity, 2, block_rows, breadth)
    incoming = lax.all_to_all(outgoing, "space", split_axis=0, concat_axis=0, tiled=True)
    incoming = incoming.reshape(devices * capacity, 2, block_rows, breadth)
    matches = (peers[:, None] == lanes[None, :]).astype(jnp.int32)
    grouped = matches.reshape(devices, per_device, devices)
    ranking = jnp.sum((jnp.cumsum(grouped, axis=1) - grouped) * grouped, axis=2)
    sender_grid = lanes[:, None] * capacity + ranking
    owned = peer_grid == position
    local_block = (targets % per_device).reshape(devices, per_device)
    where_from = (
        jnp.zeros((per_device,), jnp.int32)
        .at[jnp.where(owned, local_block, per_device).reshape(-1)]
        .set(sender_grid.reshape(-1), mode="drop")
    )
    placed = jnp.transpose(jnp.take(incoming, where_from, axis=0), (1, 0, 2, 3))
    levels = placed.reshape(2, length, height, breadth)
    wavelet_row = wavelet[0]
    receivers = receiver_cell[0]
    traces = residual[0]
    horizon = wavelet_row.shape[0]
    fields = [levels[0], levels[1]]
    adjoints = [None] * (horizon + 2)
    adjoints[horizon + 1] = adjoint_state[0, 0]
    adjoints[horizon] = adjoint_state[0, 1]
    for moment in range(1, horizon + 1):
        fields.append(
            advance(
                fields[-2],
                extend(fields[-1]),
                courant,
                wavelet_row[moment - 1 : moment],
                source_cell,
                first_row,
            )
        )
    cells = length * height * breadth
    local_cells = receivers - first_row * height * breadth
    inside = (local_cells >= 0) & (local_cells < cells)
    steps = lax.broadcasted_iota(jnp.int32, traces.shape, 0)
    spots = jnp.where(inside[None, :], local_cells[None, :], cells)
    injections = (
        jnp.zeros((horizon, cells + 1), jnp.float32)
        .at[steps, jnp.broadcast_to(spots, traces.shape)]
        .add(traces, mode="drop")
    )
    for moment in range(horizon, 0, -1):
        weighted = extend(courant * adjoints[moment])
        adjoints[moment - 1] = retreat(
            adjoints[moment + 1],
            adjoints[moment],
            weighted,
            injections[moment - 1, :cells].reshape(length, height, breadth),
        )
    partial_value = jnp.zeros((length, height, breadth), jnp.float32)
    for moment in range(1, horizon + 1):
        partial_value = partial_value + adjoints[moment] * (
            fields[moment + 1] - 2.0 * fields[moment] + fields[moment - 1]
        )
    slab_rows = partial_value.reshape(length * height, breadth)
    row_ids = lax.broadcasted_iota(jnp.int32, (1, 1, length * height), 2)
    counts = jnp.sum((check_rows[0][:, :, None] == row_ids).astype(jnp.float32), axis=1)
    check_part = jnp.dot(counts, slab_rows, precision=lax.Precision.HIGHEST)
    stacked = jnp.concatenate([partial_value, check_part[None]], axis=0)
    shot_devices = lax.axis_size("shot")
    pieces = stacked.reshape(length + 1, shot_devices, height // shot_devices, breadth)
    pieces = jnp.transpose(pieces, (1, 0, 2, 3))
    gathered = lax.all_to_all(pieces, "shot", split_axis=0, concat_axis=0, tiled=True)
    grad_share = jnp.sum(gathered[:, :length], axis=0)
    check_share = jnp.sum(gathered[:, length], axis=0)
    adjoint_carry = jnp.stack([adjoints[1], adjoints[0]])[None]
    return (grad_share, adjoint_carry, check_share[None])


def solution(mesh):
    in_specs = (
        P("space", None, None),
        P("shot", None, "space", None, None),
        P("shot", None),
        P("shot", None, "space", None, None),
        P("shot", None),
        P("shot"),
        P("shot", None),
        P("shot", None, None),
        P("space", None, None),
    )
    out_specs = (
        P("space", "shot", None),
        P("shot", None, "space", None, None),
        P("space", "shot", None),
    )
    return jax.shard_map(body, mesh=mesh, in_specs=in_specs, out_specs=out_specs, check_vma=False)
```

```python
import jax
import jax.numpy as jnp
from jax import lax
from jax.sharding import PartitionSpec as P

STENCIL = (-205.0 / 72.0, 8.0 / 5.0, -1.0 / 5.0, 8.0 / 315.0, -1.0 / 560.0)


def padded_2(array, sides, width):
    for axis, dim in sides:
        devices, length = (lax.axis_size(axis), array.shape[dim])
        up = [(i, (i + 1) % devices) for i in range(devices - 1)]
        down = [(j, i) for i, j in up]
        last = lax.slice_in_dim(array, length - width, length, axis=dim)
        initial = lax.slice_in_dim(array, 0, width, axis=dim)
        before = lax.ppermute(last, axis, up)
        after = lax.ppermute(initial, axis, down)
        array = jnp.concatenate([before, array, after], axis=dim)
    return array


def shifted(field, offset, axis):
    length = field.shape[axis]
    pad = [(0, 0)] * field.ndim
    if offset > 0:
        part = lax.slice_in_dim(field, offset, length, axis=axis)
        pad[axis] = (0, offset)
    else:
        part = lax.slice_in_dim(field, 0, length + offset, axis=axis)
        pad[axis] = (-offset, 0)
    return jnp.pad(part, pad)


def laplace(field):
    length = field.shape[0] - 8
    center = field[4 : 4 + length]
    summed = 3.0 * STENCIL[0] * center
    for offset in range(1, 5):
        summed = summed + STENCIL[offset] * (
            field[4 + offset : 4 + offset + length] + field[4 - offset : 4 - offset + length]
        )
    for axis in (1, 2):
        for offset in range(1, 5):
            summed = summed + STENCIL[offset] * (
                shifted(center, offset, axis) + shifted(center, -offset, axis)
            )
    return summed


def inject(field, cell_index, values, first_row):
    plane_cells = field.shape[1] * field.shape[2]
    local_cell = cell_index - first_row * plane_cells
    inside = (local_cell >= 0) & (local_cell < field.shape[0] * plane_cells)
    target = jnp.where(inside, local_cell, field.shape[0] * plane_cells)
    flattened = field.reshape(-1).at[target].add(values, mode="drop")
    return flattened.reshape(field.shape)


def inject_dense(field, cell_index, values, first_row):
    plane_cells = field.shape[1] * field.shape[2]
    local_cell = cell_index[0] - first_row * plane_cells
    cells = (
        lax.broadcasted_iota(jnp.int32, field.shape, 0) * plane_cells
        + lax.broadcasted_iota(jnp.int32, field.shape, 1) * field.shape[2]
        + lax.broadcasted_iota(jnp.int32, field.shape, 2)
    )
    return field + jnp.where(cells == local_cell, values[0], 0.0)


def advance(before, current_ext, courant, wave_value, source, first_row):
    following = 2.0 * current_ext[4:-4] - before + courant * laplace(current_ext)
    return inject_dense(following, source, wave_value, first_row)


def retreat(following, current, weighted_ext, injected):
    return 2.0 * current - following + laplace(weighted_ext) + injected


def extend(field):
    return padded_2(field, (("space", 0),), 4)


def body(
    courant,
    checkpoint,
    block_target,
    adjoint_state,
    wavelet,
    source_cell,
    receiver_cell,
    residual,
    check_rows,
):
    devices = lax.axis_size("space")
    position = lax.axis_index("space")
    length, height, breadth = courant.shape
    first_row = position * length
    per_device = checkpoint.shape[2]
    block_rows = checkpoint.shape[3]
    capacity = per_device // 4
    targets = block_target[0]
    payload = checkpoint[0]
    peers = targets // per_device
    lanes = jnp.arange(devices, dtype=jnp.int32)
    peer_grid = peers.reshape(devices, per_device)
    own_peers = lax.dynamic_index_in_dim(peer_grid, position, 0, keepdims=False)
    own_matches = (own_peers[:, None] == lanes[None, :]).astype(jnp.int32)
    own_ranks = jnp.sum((jnp.cumsum(own_matches, axis=0) - own_matches) * own_matches, axis=1)
    slot_of = own_peers * capacity + own_ranks
    source_of = (
        jnp.full((devices * capacity,), per_device, jnp.int32)
        .at[slot_of]
        .set(jnp.arange(per_device, dtype=jnp.int32))
    )
    by_block = jnp.transpose(payload, (1, 0, 2, 3))
    by_block = jnp.concatenate([by_block, jnp.zeros_like(by_block[:1])], axis=0)
    outgoing = jnp.take(by_block, source_of, axis=0, mode="clip")
    outgoing = outgoing.reshape(devices, capacity, 2, block_rows, breadth)
    incoming = lax.all_to_all(outgoing, "space", split_axis=0, concat_axis=0, tiled=True)
    incoming = incoming.reshape(devices * capacity, 2, block_rows, breadth)
    matches = (peers[:, None] == lanes[None, :]).astype(jnp.int32)
    grouped = matches.reshape(devices, per_device, devices)
    ranking = jnp.sum((jnp.cumsum(grouped, axis=1) - grouped) * grouped, axis=2)
    sender_grid = lanes[:, None] * capacity + ranking
    owned = peer_grid == position
    local_block = (targets % per_device).reshape(devices, per_device)
    where_from = (
        jnp.zeros((per_device,), jnp.int32)
        .at[jnp.where(owned, local_block, per_device).reshape(-1)]
        .set(sender_grid.reshape(-1), mode="drop")
    )
    placed = jnp.transpose(jnp.take(incoming, where_from, axis=0), (1, 0, 2, 3))
    levels = placed.reshape(2, length, height, breadth)
    wavelet_row = wavelet[0]
    receivers = receiver_cell[0]
    traces = residual[0]
    horizon = wavelet_row.shape[0]
    fields = [levels[0], levels[1]]
    adjoints = [None] * (horizon + 2)
    adjoints[horizon + 1] = adjoint_state[0, 0]
    adjoints[horizon] = adjoint_state[0, 1]
    for moment in range(1, horizon + 1):
        fields.append(
            advance(
                fields[-2],
                extend(fields[-1]),
                courant,
                wavelet_row[moment - 1 : moment],
                source_cell,
                first_row,
            )
        )
    cells = length * height * breadth
    local_cells = receivers - first_row * height * breadth
    inside = (local_cells >= 0) & (local_cells < cells)
    steps = lax.broadcasted_iota(jnp.int32, traces.shape, 0)
    spots = jnp.where(inside[None, :], local_cells[None, :], cells)
    injections = (
        jnp.zeros((horizon, cells + 1), jnp.float32)
        .at[steps, jnp.broadcast_to(spots, traces.shape)]
        .add(traces, mode="drop")
    )
    for moment in range(horizon, 0, -1):
        scaled = courant * adjoints[moment]
        if moment == 1:
            fields[1], scaled = lax.optimization_barrier((fields[1], scaled))
        weighted = extend(scaled)
        adjoints[moment - 1] = retreat(
            adjoints[moment + 1],
            adjoints[moment],
            weighted,
            injections[moment - 1, :cells].reshape(length, height, breadth),
        )
    partial_value = jnp.zeros((length, height, breadth), jnp.float32)
    for moment in range(1, horizon + 1):
        partial_value = partial_value + adjoints[moment] * (
            fields[moment + 1] - 2.0 * fields[moment] + fields[moment - 1]
        )
    slab_rows = partial_value.reshape(length * height, breadth)
    row_ids = lax.broadcasted_iota(jnp.int32, (1, 1, length * height), 2)
    counts = jnp.sum((check_rows[0][:, :, None] == row_ids).astype(jnp.float32), axis=1)
    check_part = jnp.dot(counts, slab_rows, precision=lax.Precision.HIGHEST)
    stacked = jnp.concatenate([partial_value, check_part[None]], axis=0)
    shot_devices = lax.axis_size("shot")
    pieces = stacked.reshape(length + 1, shot_devices, height // shot_devices, breadth)
    pieces = jnp.transpose(pieces, (1, 0, 2, 3))
    gathered = lax.all_to_all(pieces, "shot", split_axis=0, concat_axis=0, tiled=True)
    grad_share = jnp.sum(gathered[:, :length], axis=0)
    check_share = jnp.sum(gathered[:, length], axis=0)
    adjoint_carry = jnp.stack([adjoints[1], adjoints[0]])[None]
    return (grad_share, adjoint_carry, check_share[None])


def solution(mesh):
    in_specs = (
        P("space", None, None),
        P("shot", None, "space", None, None),
        P("shot", None),
        P("shot", None, "space", None, None),
        P("shot", None),
        P("shot"),
        P("shot", None),
        P("shot", None, None),
        P("space", None, None),
    )
    out_specs = (
        P("space", "shot", None),
        P("shot", None, "space", None, None),
        P("space", "shot", None),
    )
    return jax.shard_map(body, mesh=mesh, in_specs=in_specs, out_specs=out_specs, check_vma=False)
```

```python
import jax
import jax.numpy as jnp
from jax import lax
from jax.sharding import PartitionSpec as P

STENCIL = (-205.0 / 72.0, 8.0 / 5.0, -1.0 / 5.0, 8.0 / 315.0, -1.0 / 560.0)


def padded_2(array, sides, width):
    for axis, dim in sides:
        devices, length = (lax.axis_size(axis), array.shape[dim])
        up = [(i, (i + 1) % devices) for i in range(devices - 1)]
        down = [(j, i) for i, j in up]
        last = lax.slice_in_dim(array, length - width, length, axis=dim)
        initial = lax.slice_in_dim(array, 0, width, axis=dim)
        before = lax.ppermute(last, axis, up)
        after = lax.ppermute(initial, axis, down)
        array = jnp.concatenate([before, array, after], axis=dim)
    return array


def laplace(field):
    length = field.shape[0] - 8
    height = field.shape[1]
    breadth = field.shape[2]
    padded = jnp.pad(field, ((0, 0), (4, 4), (4, 4)))
    summed = 3.0 * STENCIL[0] * padded[4 : 4 + length, 4 : 4 + height, 4 : 4 + breadth]
    for offset in range(1, 5):
        summed = summed + STENCIL[offset] * (
            padded[4 + offset : 4 + offset + length, 4 : 4 + height, 4 : 4 + breadth]
            + padded[4 - offset : 4 - offset + length, 4 : 4 + height, 4 : 4 + breadth]
        )
    for offset in range(1, 5):
        summed = summed + STENCIL[offset] * (
            padded[4 : 4 + length, 4 + offset : 4 + offset + height, 4 : 4 + breadth]
            + padded[4 : 4 + length, 4 - offset : 4 - offset + height, 4 : 4 + breadth]
        )
    for offset in range(1, 5):
        summed = summed + STENCIL[offset] * (
            padded[4 : 4 + length, 4 : 4 + height, 4 + offset : 4 + offset + breadth]
            + padded[4 : 4 + length, 4 : 4 + height, 4 - offset : 4 - offset + breadth]
        )
    return summed


def inject(field, cell_index, values, first_row):
    plane_cells = field.shape[1] * field.shape[2]
    local_cell = cell_index - first_row * plane_cells
    inside = (local_cell >= 0) & (local_cell < field.shape[0] * plane_cells)
    target = jnp.where(inside, local_cell, field.shape[0] * plane_cells)
    flattened = field.reshape(-1).at[target].add(values, mode="drop")
    return flattened.reshape(field.shape)


def inject_dense(field, cell_index, values, first_row):
    plane_cells = field.shape[1] * field.shape[2]
    local_cell = cell_index[0] - first_row * plane_cells
    cells = (
        lax.broadcasted_iota(jnp.int32, field.shape, 0) * plane_cells
        + lax.broadcasted_iota(jnp.int32, field.shape, 1) * field.shape[2]
        + lax.broadcasted_iota(jnp.int32, field.shape, 2)
    )
    return field + jnp.where(cells == local_cell, values[0], 0.0)


def advance(before, current_ext, courant, wave_value, source, first_row):
    following = 2.0 * current_ext[4:-4] - before + courant * laplace(current_ext)
    return inject_dense(following, source, wave_value, first_row)


def retreat(following, current, weighted_ext, injected):
    return 2.0 * current - following + laplace(weighted_ext) + injected


def extend(field):
    return padded_2(field, (("space", 0),), 4)


def body(
    courant,
    checkpoint,
    block_target,
    adjoint_state,
    wavelet,
    source_cell,
    receiver_cell,
    residual,
    check_rows,
):
    devices = lax.axis_size("space")
    position = lax.axis_index("space")
    length, height, breadth = courant.shape
    first_row = position * length
    per_device = checkpoint.shape[2]
    block_rows = checkpoint.shape[3]
    capacity = per_device // 4
    targets = block_target[0]
    payload = checkpoint[0]
    peers = targets // per_device
    lanes = jnp.arange(devices, dtype=jnp.int32)
    peer_grid = peers.reshape(devices, per_device)
    own_peers = lax.dynamic_index_in_dim(peer_grid, position, 0, keepdims=False)
    own_matches = (own_peers[:, None] == lanes[None, :]).astype(jnp.int32)
    own_ranks = jnp.sum((jnp.cumsum(own_matches, axis=0) - own_matches) * own_matches, axis=1)
    slot_of = own_peers * capacity + own_ranks
    source_of = (
        jnp.full((devices * capacity,), per_device, jnp.int32)
        .at[slot_of]
        .set(jnp.arange(per_device, dtype=jnp.int32))
    )
    by_block = jnp.transpose(payload, (1, 0, 2, 3))
    by_block = jnp.concatenate([by_block, jnp.zeros_like(by_block[:1])], axis=0)
    outgoing = jnp.take(by_block, source_of, axis=0, mode="clip")
    outgoing = outgoing.reshape(devices, capacity, 2, block_rows, breadth)
    wavelet_row = wavelet[0]
    receivers = receiver_cell[0]
    traces = residual[0]
    horizon = wavelet_row.shape[0]
    adjoints = [None] * (horizon + 2)
    adjoints[horizon + 1] = adjoint_state[0, 0]
    adjoints[horizon] = adjoint_state[0, 1]
    cells = length * height * breadth
    local_cells = receivers - first_row * height * breadth
    inside = (local_cells >= 0) & (local_cells < cells)
    steps = lax.broadcasted_iota(jnp.int32, traces.shape, 0)
    spots = jnp.where(inside[None, :], local_cells[None, :], cells)
    injections = (
        jnp.zeros((horizon, cells + 1), jnp.float32)
        .at[steps, jnp.broadcast_to(spots, traces.shape)]
        .add(traces, mode="drop")
    )
    for moment in range(horizon, 0, -1):
        weighted = extend(courant * adjoints[moment])
        if moment == horizon - 1:
            outgoing, weighted = lax.optimization_barrier((outgoing, weighted))
        adjoints[moment - 1] = retreat(
            adjoints[moment + 1],
            adjoints[moment],
            weighted,
            injections[moment - 1, :cells].reshape(length, height, breadth),
        )
    incoming = lax.all_to_all(outgoing, "space", split_axis=0, concat_axis=0, tiled=True)
    incoming = incoming.reshape(devices * capacity, 2, block_rows, breadth)
    matches = (peers[:, None] == lanes[None, :]).astype(jnp.int32)
    grouped = matches.reshape(devices, per_device, devices)
    ranking = jnp.sum((jnp.cumsum(grouped, axis=1) - grouped) * grouped, axis=2)
    sender_grid = lanes[:, None] * capacity + ranking
    owned = peer_grid == position
    local_block = (targets % per_device).reshape(devices, per_device)
    where_from = (
        jnp.zeros((per_device,), jnp.int32)
        .at[jnp.where(owned, local_block, per_device).reshape(-1)]
        .set(sender_grid.reshape(-1), mode="drop")
    )
    placed = jnp.transpose(jnp.take(incoming, where_from, axis=0), (1, 0, 2, 3))
    levels = placed.reshape(2, length, height, breadth)
    fields = [levels[0], levels[1]]
    for moment in range(1, horizon + 1):
        fields.append(
            advance(
                fields[-2],
                extend(fields[-1]),
                courant,
                wavelet_row[moment - 1 : moment],
                source_cell,
                first_row,
            )
        )
    partial_value = jnp.zeros((length, height, breadth), jnp.float32)
    for moment in range(1, horizon + 1):
        partial_value = partial_value + adjoints[moment] * (
            fields[moment + 1] - 2.0 * fields[moment] + fields[moment - 1]
        )
    slab_rows = partial_value.reshape(length * height, breadth)
    row_ids = lax.broadcasted_iota(jnp.int32, (1, 1, length * height), 2)
    counts = jnp.sum((check_rows[0][:, :, None] == row_ids).astype(jnp.float32), axis=1)
    check_part = jnp.dot(counts, slab_rows, precision=lax.Precision.HIGHEST)
    stacked = jnp.concatenate([partial_value, check_part[None]], axis=0)
    shot_devices = lax.axis_size("shot")
    pieces = stacked.reshape(length + 1, shot_devices, height // shot_devices, breadth)
    pieces = jnp.transpose(pieces, (1, 0, 2, 3))
    gathered = lax.all_to_all(pieces, "shot", split_axis=0, concat_axis=0, tiled=True)
    grad_share = jnp.sum(gathered[:, :length], axis=0)
    check_share = jnp.sum(gathered[:, length], axis=0)
    adjoint_carry = jnp.stack([adjoints[1], adjoints[0]])[None]
    return (grad_share, adjoint_carry, check_share[None])


def solution(mesh):
    in_specs = (
        P("space", None, None),
        P("shot", None, "space", None, None),
        P("shot", None),
        P("shot", None, "space", None, None),
        P("shot", None),
        P("shot"),
        P("shot", None),
        P("shot", None, None),
        P("space", None, None),
    )
    out_specs = (
        P("space", "shot", None),
        P("shot", None, "space", None, None),
        P("space", "shot", None),
    )
    return jax.shard_map(body, mesh=mesh, in_specs=in_specs, out_specs=out_specs, check_vma=False)
```

```python
import jax
import jax.numpy as jnp
from jax import lax
from jax.sharding import PartitionSpec as P

STENCIL = (-205.0 / 72.0, 8.0 / 5.0, -1.0 / 5.0, 8.0 / 315.0, -1.0 / 560.0)


def padded_2(array, sides, width):
    for axis, dim in sides:
        devices, length = (lax.axis_size(axis), array.shape[dim])
        up = [(i, (i + 1) % devices) for i in range(devices - 1)]
        down = [(j, i) for i, j in up]
        last = lax.slice_in_dim(array, length - width, length, axis=dim)
        initial = lax.slice_in_dim(array, 0, width, axis=dim)
        before = lax.ppermute(last, axis, up)
        after = lax.ppermute(initial, axis, down)
        array = jnp.concatenate([before, array, after], axis=dim)
    return array


def laplace(field):
    length = field.shape[0] - 8
    height = field.shape[1]
    breadth = field.shape[2]
    padded = jnp.pad(field, ((0, 0), (4, 4), (4, 4)))
    summed = 3.0 * STENCIL[0] * padded[4 : 4 + length, 4 : 4 + height, 4 : 4 + breadth]
    for offset in range(1, 5):
        summed = summed + STENCIL[offset] * (
            padded[4 + offset : 4 + offset + length, 4 : 4 + height, 4 : 4 + breadth]
            + padded[4 - offset : 4 - offset + length, 4 : 4 + height, 4 : 4 + breadth]
        )
    for offset in range(1, 5):
        summed = summed + STENCIL[offset] * (
            padded[4 : 4 + length, 4 + offset : 4 + offset + height, 4 : 4 + breadth]
            + padded[4 : 4 + length, 4 - offset : 4 - offset + height, 4 : 4 + breadth]
        )
    for offset in range(1, 5):
        summed = summed + STENCIL[offset] * (
            padded[4 : 4 + length, 4 : 4 + height, 4 + offset : 4 + offset + breadth]
            + padded[4 : 4 + length, 4 : 4 + height, 4 - offset : 4 - offset + breadth]
        )
    return summed


def inject(field, cell_index, values, first_row):
    plane_cells = field.shape[1] * field.shape[2]
    local_cell = cell_index - first_row * plane_cells
    inside = (local_cell >= 0) & (local_cell < field.shape[0] * plane_cells)
    target = jnp.where(inside, local_cell, field.shape[0] * plane_cells)
    flattened = field.reshape(-1).at[target].add(values, mode="drop")
    return flattened.reshape(field.shape)


def inject_dense(field, cell_index, values, first_row):
    plane_cells = field.shape[1] * field.shape[2]
    local_cell = cell_index[0] - first_row * plane_cells
    cells = (
        lax.broadcasted_iota(jnp.int32, field.shape, 0) * plane_cells
        + lax.broadcasted_iota(jnp.int32, field.shape, 1) * field.shape[2]
        + lax.broadcasted_iota(jnp.int32, field.shape, 2)
    )
    return field + jnp.where(cells == local_cell, values[0], 0.0)


def advance(before, current_ext, courant, wave_value, source, first_row):
    following = 2.0 * current_ext[4:-4] - before + courant * laplace(current_ext)
    return inject_dense(following, source, wave_value, first_row)


def retreat(following, current, weighted_ext, injected):
    return 2.0 * current - following + laplace(weighted_ext) + injected


def extend(field):
    return padded_2(field, (("space", 0),), 4)


def body(
    courant,
    checkpoint,
    block_target,
    adjoint_state,
    wavelet,
    source_cell,
    receiver_cell,
    residual,
    check_rows,
):
    devices = lax.axis_size("space")
    position = lax.axis_index("space")
    length, height, breadth = courant.shape
    first_row = position * length
    per_device = checkpoint.shape[2]
    block_rows = checkpoint.shape[3]
    capacity = per_device // 4
    targets = block_target[0]
    payload = checkpoint[0]
    peers = targets // per_device
    lanes = jnp.arange(devices, dtype=jnp.int32)
    peer_grid = peers.reshape(devices, per_device)
    own_peers = lax.dynamic_index_in_dim(peer_grid, position, 0, keepdims=False)
    own_matches = (own_peers[:, None] == lanes[None, :]).astype(jnp.int32)
    own_ranks = jnp.sum((jnp.cumsum(own_matches, axis=0) - own_matches) * own_matches, axis=1)
    slot_of = own_peers * capacity + own_ranks
    source_of = (
        jnp.full((devices * capacity,), per_device, jnp.int32)
        .at[slot_of]
        .set(jnp.arange(per_device, dtype=jnp.int32))
    )
    by_block = jnp.transpose(payload, (1, 0, 2, 3))
    by_block = jnp.concatenate([by_block, jnp.zeros_like(by_block[:1])], axis=0)
    outgoing = jnp.take(by_block, source_of, axis=0, mode="clip")
    outgoing = outgoing.reshape(devices, capacity, 2, block_rows, breadth)
    incoming = lax.all_to_all(outgoing, "space", split_axis=0, concat_axis=0, tiled=True)
    incoming = incoming.reshape(devices * capacity, 2, block_rows, breadth)
    matches = (peers[:, None] == lanes[None, :]).astype(jnp.int32)
    grouped = matches.reshape(devices, per_device, devices)
    ranking = jnp.sum((jnp.cumsum(grouped, axis=1) - grouped) * grouped, axis=2)
    sender_grid = lanes[:, None] * capacity + ranking
    owned = peer_grid == position
    local_block = (targets % per_device).reshape(devices, per_device)
    where_from = (
        jnp.zeros((per_device,), jnp.int32)
        .at[jnp.where(owned, local_block, per_device).reshape(-1)]
        .set(sender_grid.reshape(-1), mode="drop")
    )
    placed = jnp.transpose(jnp.take(incoming, where_from, axis=0), (1, 0, 2, 3))
    levels = placed.reshape(2, length, height, breadth)
    wavelet_row = wavelet[0]
    receivers = receiver_cell[0]
    traces = residual[0]
    horizon = wavelet_row.shape[0]
    fields = [levels[0], levels[1]]
    adjoints = [None] * (horizon + 2)
    adjoints[horizon + 1] = adjoint_state[0, 0]
    adjoints[horizon] = adjoint_state[0, 1]
    for moment in range(1, horizon):
        fields.append(
            advance(
                fields[-2],
                extend(fields[-1]),
                courant,
                wavelet_row[moment - 1 : moment],
                source_cell,
                first_row,
            )
        )
    last_curvature = inject_dense(
        courant * laplace(extend(fields[-1])), source_cell, wavelet_row[horizon - 1 :], first_row
    )
    cells = length * height * breadth
    local_cells = receivers - first_row * height * breadth
    inside = (local_cells >= 0) & (local_cells < cells)
    steps = lax.broadcasted_iota(jnp.int32, traces.shape, 0)
    spots = jnp.where(inside[None, :], local_cells[None, :], cells)
    injections = (
        jnp.zeros((horizon, cells + 1), jnp.float32)
        .at[steps, jnp.broadcast_to(spots, traces.shape)]
        .add(traces, mode="drop")
    )
    for moment in range(horizon, 0, -1):
        weighted = extend(courant * adjoints[moment])
        adjoints[moment - 1] = retreat(
            adjoints[moment + 1],
            adjoints[moment],
            weighted,
            injections[moment - 1, :cells].reshape(length, height, breadth),
        )
    partial_value = jnp.zeros((length, height, breadth), jnp.float32)
    for moment in range(1, horizon):
        partial_value = partial_value + adjoints[moment] * (
            fields[moment + 1] - 2.0 * fields[moment] + fields[moment - 1]
        )
    partial_value = partial_value + adjoints[horizon] * last_curvature
    slab_rows = partial_value.reshape(length * height, breadth)
    row_ids = lax.broadcasted_iota(jnp.int32, (1, 1, length * height), 2)
    counts = jnp.sum((check_rows[0][:, :, None] == row_ids).astype(jnp.float32), axis=1)
    check_part = jnp.dot(counts, slab_rows, precision=lax.Precision.HIGHEST)
    stacked = jnp.concatenate([partial_value, check_part[None]], axis=0)
    shot_devices = lax.axis_size("shot")
    pieces = stacked.reshape(length + 1, shot_devices, height // shot_devices, breadth)
    pieces = jnp.transpose(pieces, (1, 0, 2, 3))
    gathered = lax.all_to_all(pieces, "shot", split_axis=0, concat_axis=0, tiled=True)
    grad_share = jnp.sum(gathered[:, :length], axis=0)
    check_share = jnp.sum(gathered[:, length], axis=0)
    adjoint_carry = jnp.stack([adjoints[1], adjoints[0]])[None]
    return (grad_share, adjoint_carry, check_share[None])


def solution(mesh):
    in_specs = (
        P("space", None, None),
        P("shot", None, "space", None, None),
        P("shot", None),
        P("shot", None, "space", None, None),
        P("shot", None),
        P("shot"),
        P("shot", None),
        P("shot", None, None),
        P("space", None, None),
    )
    out_specs = (
        P("space", "shot", None),
        P("shot", None, "space", None, None),
        P("space", "shot", None),
    )
    return jax.shard_map(body, mesh=mesh, in_specs=in_specs, out_specs=out_specs, check_vma=False)
```

```python
import jax
import jax.numpy as jnp
from jax import lax
from jax.sharding import PartitionSpec as P

STENCIL = (-205.0 / 72.0, 8.0 / 5.0, -1.0 / 5.0, 8.0 / 315.0, -1.0 / 560.0)


def padded_2(array, sides, width):
    for axis, dim in sides:
        devices, length = (lax.axis_size(axis), array.shape[dim])
        up = [(i, (i + 1) % devices) for i in range(devices - 1)]
        down = [(j, i) for i, j in up]
        last = lax.slice_in_dim(array, length - width, length, axis=dim)
        initial = lax.slice_in_dim(array, 0, width, axis=dim)
        before = lax.ppermute(last, axis, up)
        after = lax.ppermute(initial, axis, down)
        array = jnp.concatenate([before, array, after], axis=dim)
    return array


def laplace(field):
    length = field.shape[0] - 8
    height = field.shape[1]
    breadth = field.shape[2]
    padded = jnp.pad(field, ((0, 0), (4, 4), (4, 4)))
    summed = 3.0 * STENCIL[0] * padded[4 : 4 + length, 4 : 4 + height, 4 : 4 + breadth]
    for offset in range(1, 5):
        summed = summed + STENCIL[offset] * (
            padded[4 + offset : 4 + offset + length, 4 : 4 + height, 4 : 4 + breadth]
            + padded[4 - offset : 4 - offset + length, 4 : 4 + height, 4 : 4 + breadth]
        )
    for offset in range(1, 5):
        summed = summed + STENCIL[offset] * (
            padded[4 : 4 + length, 4 + offset : 4 + offset + height, 4 : 4 + breadth]
            + padded[4 : 4 + length, 4 - offset : 4 - offset + height, 4 : 4 + breadth]
        )
    for offset in range(1, 5):
        summed = summed + STENCIL[offset] * (
            padded[4 : 4 + length, 4 : 4 + height, 4 + offset : 4 + offset + breadth]
            + padded[4 : 4 + length, 4 : 4 + height, 4 - offset : 4 - offset + breadth]
        )
    return summed


def inject(field, cell_index, values, first_row):
    plane_cells = field.shape[1] * field.shape[2]
    local_cell = cell_index - first_row * plane_cells
    inside = (local_cell >= 0) & (local_cell < field.shape[0] * plane_cells)
    target = jnp.where(inside, local_cell, field.shape[0] * plane_cells)
    flattened = field.reshape(-1).at[target].add(values, mode="drop")
    return flattened.reshape(field.shape)


def inject_dense(field, cell_index, values, first_row):
    plane_cells = field.shape[1] * field.shape[2]
    local_cell = cell_index[0] - first_row * plane_cells
    cells = (
        lax.broadcasted_iota(jnp.int32, field.shape, 0) * plane_cells
        + lax.broadcasted_iota(jnp.int32, field.shape, 1) * field.shape[2]
        + lax.broadcasted_iota(jnp.int32, field.shape, 2)
    )
    return field + jnp.where(cells == local_cell, values[0], 0.0)


def advance(before, current_ext, courant, wave_value, source, first_row):
    following = 2.0 * current_ext[4:-4] - before + courant * laplace(current_ext)
    return inject_dense(following, source, wave_value, first_row)


def retreat(following, current, weighted_ext, injected):
    return 2.0 * current - following + laplace(weighted_ext) + injected


def extend(field):
    return padded_2(field, (("space", 0),), 4)


def body(
    courant,
    checkpoint,
    block_target,
    adjoint_state,
    wavelet,
    source_cell,
    receiver_cell,
    residual,
    check_rows,
):
    devices = lax.axis_size("space")
    position = lax.axis_index("space")
    length, height, breadth = courant.shape
    first_row = position * length
    per_device = checkpoint.shape[2]
    block_rows = checkpoint.shape[3]
    capacity = per_device // 4
    targets = block_target[0]
    payload = checkpoint[0]
    peers = targets // per_device
    lanes = jnp.arange(devices, dtype=jnp.int32)
    peer_grid = peers.reshape(devices, per_device)
    own_peers = lax.dynamic_index_in_dim(peer_grid, position, 0, keepdims=False)
    own_matches = (own_peers[:, None] == lanes[None, :]).astype(jnp.int32)
    own_ranks = jnp.sum((jnp.cumsum(own_matches, axis=0) - own_matches) * own_matches, axis=1)
    slot_of = own_peers * capacity + own_ranks
    source_of = (
        jnp.full((devices * capacity,), per_device, jnp.int32)
        .at[slot_of]
        .set(jnp.arange(per_device, dtype=jnp.int32))
    )
    by_block = jnp.transpose(payload, (1, 0, 2, 3))
    by_block = jnp.concatenate([by_block, jnp.zeros_like(by_block[:1])], axis=0)
    outgoing = jnp.take(by_block, source_of, axis=0, mode="clip")
    outgoing = outgoing.reshape(devices, capacity, 2, block_rows, breadth)
    incoming = lax.all_to_all(outgoing, "space", split_axis=0, concat_axis=0, tiled=True)
    incoming = incoming.reshape(devices * capacity, 2, block_rows, breadth)
    matches = (peers[:, None] == lanes[None, :]).astype(jnp.int32)
    grouped = matches.reshape(devices, per_device, devices)
    ranking = jnp.sum((jnp.cumsum(grouped, axis=1) - grouped) * grouped, axis=2)
    sender_grid = lanes[:, None] * capacity + ranking
    owned = peer_grid == position
    local_block = (targets % per_device).reshape(devices, per_device)
    where_from = (
        jnp.zeros((per_device,), jnp.int32)
        .at[jnp.where(owned, local_block, per_device).reshape(-1)]
        .set(sender_grid.reshape(-1), mode="drop")
    )
    placed = jnp.transpose(jnp.take(incoming, where_from, axis=0), (1, 0, 2, 3))
    levels = placed.reshape(2, length, height, breadth)
    wavelet_row = wavelet[0]
    receivers = receiver_cell[0]
    traces = residual[0]
    horizon = wavelet_row.shape[0]
    fields = [levels[0], levels[1]]
    adjoints = [None] * (horizon + 2)
    adjoints[horizon + 1] = adjoint_state[0, 0]
    adjoints[horizon] = adjoint_state[0, 1]
    for moment in range(1, horizon + 1):
        fields.append(
            advance(
                fields[-2],
                extend(fields[-1]),
                courant,
                wavelet_row[moment - 1 : moment],
                source_cell,
                first_row,
            )
        )
    cells = length * height * breadth
    local_cells = receivers - first_row * height * breadth
    inside = (local_cells >= 0) & (local_cells < cells)
    steps = lax.broadcasted_iota(jnp.int32, traces.shape, 0)
    spots = jnp.where(inside[None, :], local_cells[None, :], cells)
    injections = (
        jnp.zeros((horizon, cells + 1), jnp.float32)
        .at[steps, jnp.broadcast_to(spots, traces.shape)]
        .add(traces, mode="drop")
    )
    for moment in range(horizon, 0, -1):
        weighted = extend(courant * adjoints[moment])
        adjoints[moment - 1] = retreat(
            adjoints[moment + 1],
            adjoints[moment],
            weighted,
            injections[moment - 1, :cells].reshape(length, height, breadth),
        )
    partial_value = jnp.zeros((length, height, breadth), jnp.float32)
    for moment in range(1, horizon + 1):
        partial_value = partial_value + adjoints[moment] * (
            fields[moment + 1] - 2.0 * fields[moment] + fields[moment - 1]
        )
    slab_rows = partial_value.reshape(length * height, breadth)
    row_ids = lax.broadcasted_iota(jnp.int32, (1, 1, length * height), 2)
    counts = jnp.sum((check_rows[0][:, :, None] == row_ids).astype(jnp.float32), axis=1)
    check_part = jnp.dot(counts, slab_rows, precision=lax.Precision.HIGHEST)
    stacked = jnp.concatenate([partial_value, check_part[None]], axis=0)
    shot_devices = lax.axis_size("shot")
    pieces = stacked.reshape(length + 1, shot_devices, height // shot_devices, breadth)
    pieces = jnp.transpose(pieces, (1, 0, 2, 3))
    gathered = lax.all_to_all(pieces, "shot", split_axis=0, concat_axis=0, tiled=True)
    shares = jnp.sum(gathered, axis=0)
    grad_share = shares[:length]
    check_share = shares[length]
    adjoint_carry = jnp.stack([adjoints[1], adjoints[0]])[None]
    return (grad_share, adjoint_carry, check_share[None])


def solution(mesh):
    in_specs = (
        P("space", None, None),
        P("shot", None, "space", None, None),
        P("shot", None),
        P("shot", None, "space", None, None),
        P("shot", None),
        P("shot"),
        P("shot", None),
        P("shot", None, None),
        P("space", None, None),
    )
    out_specs = (
        P("space", "shot", None),
        P("shot", None, "space", None, None),
        P("space", "shot", None),
    )
    return jax.shard_map(body, mesh=mesh, in_specs=in_specs, out_specs=out_specs, check_vma=False)
```

```python
import jax
import jax.numpy as jnp
from jax import lax
from jax.sharding import PartitionSpec as P

STENCIL = (-205.0 / 72.0, 8.0 / 5.0, -1.0 / 5.0, 8.0 / 315.0, -1.0 / 560.0)


def padded_2(array, sides, width):
    for axis, dim in sides:
        devices, length = (lax.axis_size(axis), array.shape[dim])
        up = [(i, (i + 1) % devices) for i in range(devices - 1)]
        down = [(j, i) for i, j in up]
        last = lax.slice_in_dim(array, length - width, length, axis=dim)
        initial = lax.slice_in_dim(array, 0, width, axis=dim)
        before = lax.ppermute(last, axis, up)
        after = lax.ppermute(initial, axis, down)
        array = jnp.concatenate([before, array, after], axis=dim)
    return array


def laplace(field):
    length = field.shape[0] - 8
    height = field.shape[1]
    breadth = field.shape[2]
    padded = jnp.pad(field, ((0, 0), (4, 4), (4, 4)))
    summed = 3.0 * STENCIL[0] * padded[4 : 4 + length, 4 : 4 + height, 4 : 4 + breadth]
    for offset in range(1, 5):
        summed = summed + STENCIL[offset] * (
            padded[4 + offset : 4 + offset + length, 4 : 4 + height, 4 : 4 + breadth]
            + padded[4 - offset : 4 - offset + length, 4 : 4 + height, 4 : 4 + breadth]
        )
    for offset in range(1, 5):
        summed = summed + STENCIL[offset] * (
            padded[4 : 4 + length, 4 + offset : 4 + offset + height, 4 : 4 + breadth]
            + padded[4 : 4 + length, 4 - offset : 4 - offset + height, 4 : 4 + breadth]
        )
    for offset in range(1, 5):
        summed = summed + STENCIL[offset] * (
            padded[4 : 4 + length, 4 : 4 + height, 4 + offset : 4 + offset + breadth]
            + padded[4 : 4 + length, 4 : 4 + height, 4 - offset : 4 - offset + breadth]
        )
    return summed


def inject(field, cell_index, values, first_row):
    plane_cells = field.shape[1] * field.shape[2]
    local_cell = cell_index - first_row * plane_cells
    inside = (local_cell >= 0) & (local_cell < field.shape[0] * plane_cells)
    target = jnp.where(inside, local_cell, field.shape[0] * plane_cells)
    flattened = field.reshape(-1).at[target].add(values, mode="drop")
    return flattened.reshape(field.shape)


def inject_dense(field, cell_index, values, first_row):
    plane_cells = field.shape[1] * field.shape[2]
    local_cell = cell_index[0] - first_row * plane_cells
    cells = (
        lax.broadcasted_iota(jnp.int32, field.shape, 0) * plane_cells
        + lax.broadcasted_iota(jnp.int32, field.shape, 1) * field.shape[2]
        + lax.broadcasted_iota(jnp.int32, field.shape, 2)
    )
    return field + jnp.where(cells == local_cell, values[0], 0.0)


def advance(before, current_ext, courant, wave_value, source, first_row):
    following = 2.0 * current_ext[4:-4] - before + courant * laplace(current_ext)
    return inject_dense(following, source, wave_value, first_row)


def retreat(following, current, weighted_ext, injected):
    return 2.0 * current - following + laplace(weighted_ext) + injected


def extend(field):
    return padded_2(field, (("space", 0),), 4)


def body(
    courant,
    checkpoint,
    block_target,
    adjoint_state,
    wavelet,
    source_cell,
    receiver_cell,
    residual,
    check_rows,
):
    devices = lax.axis_size("space")
    position = lax.axis_index("space")
    length, height, breadth = courant.shape
    first_row = position * length
    per_device = checkpoint.shape[2]
    block_rows = checkpoint.shape[3]
    capacity = per_device // 4
    targets = block_target[0]
    payload = checkpoint[0]
    peers = targets // per_device
    lanes = jnp.arange(devices, dtype=jnp.int32)
    peer_grid = peers.reshape(devices, per_device)
    own_peers = lax.dynamic_index_in_dim(peer_grid, position, 0, keepdims=False)
    own_matches = (own_peers[:, None] == lanes[None, :]).astype(jnp.int32)
    own_ranks = jnp.sum((jnp.cumsum(own_matches, axis=0) - own_matches) * own_matches, axis=1)
    slot_of = own_peers * capacity + own_ranks
    source_of = (
        jnp.full((devices * capacity,), per_device, jnp.int32)
        .at[slot_of]
        .set(jnp.arange(per_device, dtype=jnp.int32))
    )
    by_block = jnp.transpose(payload, (1, 0, 2, 3))
    by_block = jnp.concatenate([by_block, jnp.zeros_like(by_block[:1])], axis=0)
    outgoing = jnp.take(by_block, source_of, axis=0, mode="clip")
    outgoing = outgoing.reshape(devices, capacity, 2, block_rows, breadth)
    incoming = lax.all_to_all(outgoing, "space", split_axis=0, concat_axis=0, tiled=True)
    incoming = incoming.reshape(devices * capacity, 2, block_rows, breadth)
    matches = (peers[:, None] == lanes[None, :]).astype(jnp.int32)
    grouped = matches.reshape(devices, per_device, devices)
    ranking = jnp.sum((jnp.cumsum(grouped, axis=1) - grouped) * grouped, axis=2)
    sender_grid = lanes[:, None] * capacity + ranking
    owned = peer_grid == position
    local_block = (targets % per_device).reshape(devices, per_device)
    where_from = (
        jnp.zeros((per_device,), jnp.int32)
        .at[jnp.where(owned, local_block, per_device).reshape(-1)]
        .set(sender_grid.reshape(-1), mode="drop")
    )
    placed = jnp.transpose(jnp.take(incoming, where_from, axis=0, mode="clip"), (1, 0, 2, 3))
    levels = placed.reshape(2, length, height, breadth)
    wavelet_row = wavelet[0]
    receivers = receiver_cell[0]
    traces = residual[0]
    horizon = wavelet_row.shape[0]
    fields = [levels[0], levels[1]]
    adjoints = [None] * (horizon + 2)
    adjoints[horizon + 1] = adjoint_state[0, 0]
    adjoints[horizon] = adjoint_state[0, 1]
    for moment in range(1, horizon + 1):
        fields.append(
            advance(
                fields[-2],
                extend(fields[-1]),
                courant,
                wavelet_row[moment - 1 : moment],
                source_cell,
                first_row,
            )
        )
    cells = length * height * breadth
    local_cells = receivers - first_row * height * breadth
    inside = (local_cells >= 0) & (local_cells < cells)
    steps = lax.broadcasted_iota(jnp.int32, traces.shape, 0)
    spots = jnp.where(inside[None, :], local_cells[None, :], cells)
    injections = (
        jnp.zeros((horizon, cells + 1), jnp.float32)
        .at[steps, jnp.broadcast_to(spots, traces.shape)]
        .add(traces, mode="drop")
    )
    for moment in range(horizon, 0, -1):
        weighted = extend(courant * adjoints[moment])
        adjoints[moment - 1] = retreat(
            adjoints[moment + 1],
            adjoints[moment],
            weighted,
            injections[moment - 1, :cells].reshape(length, height, breadth),
        )
    partial_value = jnp.zeros((length, height, breadth), jnp.float32)
    for moment in range(1, horizon + 1):
        partial_value = partial_value + adjoints[moment] * (
            fields[moment + 1] - 2.0 * fields[moment] + fields[moment - 1]
        )
    slab_rows = partial_value.reshape(length * height, breadth)
    row_ids = lax.broadcasted_iota(jnp.int32, (1, 1, length * height), 2)
    counts = jnp.sum((check_rows[0][:, :, None] == row_ids).astype(jnp.float32), axis=1)
    check_part = jnp.dot(counts, slab_rows, precision=lax.Precision.HIGHEST)
    stacked = jnp.concatenate([partial_value, check_part[None]], axis=0)
    shot_devices = lax.axis_size("shot")
    pieces = stacked.reshape(length + 1, shot_devices, height // shot_devices, breadth)
    pieces = jnp.transpose(pieces, (1, 0, 2, 3))
    gathered = lax.all_to_all(pieces, "shot", split_axis=0, concat_axis=0, tiled=True)
    shares = jnp.sum(gathered, axis=0)
    grad_share = shares[:length]
    check_share = shares[length]
    adjoint_carry = jnp.stack([adjoints[1], adjoints[0]])[None]
    return (grad_share, adjoint_carry, check_share[None])


def solution(mesh):
    in_specs = (
        P("space", None, None),
        P("shot", None, "space", None, None),
        P("shot", None),
        P("shot", None, "space", None, None),
        P("shot", None),
        P("shot"),
        P("shot", None),
        P("shot", None, None),
        P("space", None, None),
    )
    out_specs = (
        P("space", "shot", None),
        P("shot", None, "space", None, None),
        P("space", "shot", None),
    )
    return jax.shard_map(body, mesh=mesh, in_specs=in_specs, out_specs=out_specs, check_vma=False)
```
